32 devices in a mesh: snp: 8 (over z, y), ind: 4 (over x, core).
Axes of the slice: x: 2, y: 2, z: 4, core: 2. Of those that a mesh axis runs over, the one named last changes fastest.
Arguments:
- beta_hat: float32 [64, 8192], P('ind', 'snp'), may hold values from -8 to 8
- ld_band: float32 [8192, 1024], P('snp'), as said below
- band_start: int32 [64], P('snp'), may hold values from -480 to 7648, as said below
- heritability: float32 [64], P('ind'), may hold values from 0.2 to 0.6
- genotypes: bfloat16 [4096, 8192], P('ind', 'snp'), may hold values from 0 to 2, as said below
Outputs:
- weights: float32 [64, 8192], P('ind', 'snp')
- scores: float32 [64, 4096], P(None, ('ind', 'snp'))
The draws below stay inside these ranges and needn't reach their ends.
Inputs may be any that keep to these rules, and one draw needn't show every extreme that they name: ld_band is a symmetric matrix R in band form: entry k of row i is R[i, band_start[i // 128] + k]; R[i, i] = 1; R[i, j] = 0 when |i - j| > 416 or j lies outside the SNPs; the off-diagonal magnitudes of a row sum to 2.5 at most. `band_start`: block b's window starts at 128 * b - 416 - k with k from 0 to 64; the first block has k = 64 and the last block k = 0. `genotypes`: dosages are 0, 1 or 2.
All inputs are finite; a program needn't handle non-finite values.
Results may differ from the reference program's by a relative error of at most 0.0021.
Values may be sent and summed in bfloat16 or wider, within the bound.
No kernel may reach another device: no remote copies, remote signals or barrier semaphores. Data moves between devices by JAX's collectives and lax.ppermute only.
A program may use at most 64 MiB of HBM per device.

```python
import math
import jax
import jax.numpy as jnp
from jax import lax

TRAITS = 64
BW = 1024
BLK = 128
ITERS = 2
M_GENOME = 1100000
N_GWAS = 1000000
IND_DEV = 1024
REACH = 416
M = 8192
IND = 4096


def window_starts(key):
    block_count = M // BLK
    slack_cols = BW - BLK - 2 * REACH
    sub_key = jax.random.fold_in(key, 11)
    key_offsets, key_pick = jax.random.split(sub_key)
    offsets = jax.random.randint(key_offsets, (block_count,), 0, slack_cols + 1)
    chosen = jax.random.permutation(key_pick, block_count)
    offsets = offsets.at[chosen[0]].set(0).at[chosen[1]].set(slack_cols)
    offsets = offsets.at[0].set(slack_cols).at[block_count - 1].set(0)
    return (jnp.arange(block_count, dtype=jnp.int32) * BLK - REACH - offsets).astype(jnp.int32)


def draw_band_start(key, part):
    return window_starts(key)


def draw_ld_band(key, part):
    starts = window_starts(key)
    table_key = jax.random.fold_in(key, 23)
    table = jax.random.uniform(table_key, (M, REACH + 1), jnp.float32, 0.5, 1.0)
    reach_float = float(REACH)
    distances = jnp.arange(1, REACH + 1, dtype=jnp.float32)
    scale = 1.25 / jnp.sum(1.0 / (1.0 + distances / reach_float))
    row_ids = jnp.arange(M, dtype=jnp.int32)[:, None]
    col_ids = jnp.repeat(starts, BLK)[:, None] + jnp.arange(BW, dtype=jnp.int32)[None, :]
    gap = jnp.abs(row_ids - col_ids)
    anchor = jnp.clip(jnp.minimum(row_ids, col_ids), 0, M - 1)
    picked = table[anchor, jnp.clip(gap, 0, REACH)]
    entries = scale * picked / (1.0 + gap.astype(jnp.float32) / reach_float)
    inside = (gap <= REACH) & (col_ids >= 0) & (col_ids < M)
    return jnp.where(gap == 0, 1.0, jnp.where(inside, entries, 0.0)).astype(jnp.float32)


def draw_beta_hat(key, part):
    sub_key = jax.random.fold_in(key, 53)
    keys = jax.random.split(sub_key, 6)
    positions = jnp.arange(M, dtype=jnp.float32)
    wave_lengths = 4.0 * REACH * jnp.exp(jax.random.uniform(keys[0], (TRAITS, 6), jnp.float32, 0.0, math.log(8.0)))
    angular = 2.0 * math.pi / wave_lengths
    phases = jax.random.uniform(keys[1], (TRAITS, 6), jnp.float32, 0.0, 2.0 * math.pi)
    coefs = 0.5 * jax.random.normal(keys[2], (TRAITS, 6), jnp.float32)
    smooth = jnp.zeros((TRAITS, M), jnp.float32)
    for term in range(6):
        smooth = smooth + coefs[:, term:term + 1] * jnp.cos(positions[None, :] * angular[:, term:term + 1] + phases[:, term:term + 1])
    region_count = M // BW + 1
    region_amp = jnp.exp(jax.random.uniform(keys[3], (TRAITS, region_count), jnp.float32, math.log(0.2), math.log(2.5)))
    trait_amp = jnp.exp(jax.random.uniform(keys[4], (TRAITS, 1), jnp.float32, math.log(0.3), math.log(1.5)))
    region_index = jnp.arange(M, dtype=jnp.int32) // BW
    envelope = trait_amp * jnp.take(region_amp, region_index, axis=1)
    noise = jax.random.normal(keys[5], (TRAITS, M), jnp.float32)
    return jnp.clip(envelope * smooth + noise, -8.0, 8.0).astype(jnp.float32)


def draw_genotypes(key, part):
    sub_key = jax.random.fold_in(key, 37)
    base_key, dose_key = jax.random.split(sub_key)
    base = jax.random.uniform(base_key, (M,), jnp.float32, 0.04, 0.12)

    def row_block(block_index):
        rows_key = jax.random.fold_in(dose_key, block_index)
        uniforms = jax.random.uniform(rows_key, (2, IND_DEV, M), jnp.float32)
        person = (block_index * IND_DEV + jnp.arange(IND_DEV)).astype(jnp.float32)
        chance = base[None, :] * (1.0 + 3.0 * person / IND)[:, None]
        return jnp.sum((uniforms < chance[None]).astype(jnp.float32), axis=0).astype(jnp.bfloat16)
    blocks = lax.map(row_block, jnp.arange(IND // IND_DEV))
    return blocks.reshape(IND, M)


def steps_of(own_key, shape, pieces, least, high):
    level, own = 1.0, jax.random.fold_in(own_key, 6)
    for axis_at, blocks in pieces:
        heights = jnp.exp(jax.random.uniform(jax.random.fold_in(own, axis_at), (blocks,), jnp.float32, least / len(pieces), high / len(pieces)))
        level = level * jnp.repeat(heights, shape[axis_at] // blocks).reshape([-1 if axis == axis_at else 1 for axis in range(len(shape))])
    return level


def setup_inputs(seed: int = 0) -> dict:
    arg_keys = jax.random.split(jax.random.key(seed), 6)
    beta_hat = draw_beta_hat(jax.random.fold_in(arg_keys[5], 71), 0)
    ld_band = draw_ld_band(jax.random.fold_in(arg_keys[5], 71), 0)
    band_start = draw_band_start(jax.random.fold_in(arg_keys[5], 71), 0)
    heritability = jnp.clip(jnp.exp(math.log(0.6) - 1.0986123 * jax.random.uniform(arg_keys[3], (TRAITS,), jnp.float32) ** steps_of(arg_keys[3], (TRAITS,), ((0, 4),), -0.2, 0.2)), 0.2, 0.6)
    genotypes = draw_genotypes(jax.random.fold_in(arg_keys[5], 71), 0)
    return {"beta_hat": beta_hat, "ld_band": ld_band, "band_start": band_start, "heritability": heritability, "genotypes": genotypes}


def apply_operator(vector, ld_band, band_start, ridge_shift):
    halo_cols = BW - BLK
    padded = jnp.pad(vector, ((0, 0), (halo_cols, halo_cols)))
    blocks = ld_band.reshape(M // BLK, BLK, BW)

    def one_block(pair_item):
        first_col, band_rows = pair_item
        window = lax.dynamic_slice_in_dim(padded, (first_col + halo_cols).astype(jnp.int32), BW, 1)
        return jnp.dot(window, band_rows.T, precision=lax.Precision.HIGHEST)
    block_out = lax.map(one_block, (band_start, blocks))
    product = jnp.transpose(block_out, (1, 0, 2)).reshape(vector.shape[0], M)
    return product + ridge_shift[:, None] * vector

def reference(beta_hat, ld_band, band_start, heritability, genotypes):
    ridge_shift = M_GENOME / N_GWAS / heritability
    weights = jnp.zeros_like(beta_hat)
    residual = beta_hat
    direction = beta_hat
    norm_now = lax.optimization_barrier(jnp.sum(residual * residual, axis=1))
    for turn_index in range(ITERS):
        product = apply_operator(direction, ld_band, band_start, ridge_shift)
        step_size = norm_now / lax.optimization_barrier(jnp.sum(direction * product, axis=1))
        weights = weights + step_size[:, None] * direction
        residual = residual - step_size[:, None] * product
        if turn_index + 1 < ITERS:
            norm_next = lax.optimization_barrier(jnp.sum(residual * residual, axis=1))
            direction = residual + (norm_next / norm_now)[:, None] * direction
            norm_now = norm_next
    rounded = weights.astype(jnp.bfloat16)
    raw_scores = lax.dot_general(rounded, genotypes, (((1,), (1,)), ((), ())), preferred_element_type=jnp.float32)
    average = lax.optimization_barrier(jnp.sum(raw_scores, axis=1)) / raw_scores.shape[1]
    centred = raw_scores - average[:, None]
    variance = lax.optimization_barrier(jnp.sum(centred * centred, axis=1)) / raw_scores.shape[1]
    scores = centred * lax.rsqrt(variance + 1e-05)[:, None]
    return (weights, scores)
```

```python
import jax
import jax.numpy as jnp
from jax import lax
from jax.sharding import PartitionSpec as P

BLK = 128
ITERS = 2
M_GENOME = 1100000
N_GWAS = 1000000
REACH = 416
SHIFT_BITS = 7


def all_sum(x, axes, count):
    sent = jnp.broadcast_to(x[None], (count,) + x.shape)
    return jnp.sum(lax.all_to_all(sent, axes, 0, 0, tiled=True), axis=0)


def with_halo(block, width):
    count = lax.axis_size("snp")
    forward = [(i, i + 1) for i in range(count - 1)]
    backward = [(target, source) for source, target in forward]
    low = lax.ppermute(block[:, block.shape[1] - width :], "snp", forward)
    high = lax.ppermute(block[:, :width], "snp", backward)
    return jnp.concatenate([low, block, high], axis=1)


def apply_operator(vector, ld_band, shifts, ridge_shift, halo):
    band_cols = ld_band.shape[1]
    blocks_here = ld_band.shape[0] // BLK
    span = band_cols + (1 << SHIFT_BITS) - 1
    padded = with_halo(vector, halo)
    need = (blocks_here - 1) * BLK + span
    padded = jnp.pad(padded, ((0, 0), (0, max(0, need - padded.shape[1]))))
    wide = jnp.stack([padded[:, b * BLK : b * BLK + span] for b in range(blocks_here)])
    for bit in range(SHIFT_BITS):
        step = 1 << bit
        take = ((shifts >> bit) & 1)[:, None, None] == 1
        wide = jnp.where(take, wide[:, :, step:], wide[:, :, :-step])
    windows = wide[:, :, :band_cols]
    blocks = ld_band.reshape(blocks_here, BLK, band_cols)
    product = jnp.einsum("btk,brk->tbr", windows, blocks, precision=lax.Precision.HIGHEST)
    return product.reshape(vector.shape) + ridge_shift[:, None] * vector


def local(beta_hat, ld_band, band_start, heritability, genotypes):
    n_snp = lax.axis_size("snp")
    n_ind = lax.axis_size("ind")
    n_all = n_snp * n_ind
    me_ind = lax.axis_index("ind")
    traits_here, rows_here = beta_hat.shape
    traits = traits_here * n_ind
    halo = ld_band.shape[1] - BLK - REACH
    offsets = band_start - lax.axis_index("snp") * rows_here + halo
    shifts = offsets - jnp.arange(band_start.shape[0], dtype=jnp.int32) * BLK

    ridge_shift = M_GENOME / N_GWAS / heritability
    colsum = jnp.sum(genotypes.astype(jnp.float32), axis=0)
    colsum = all_sum(colsum, "ind", n_ind)
    beta_all = lax.all_gather(beta_hat, "ind", axis=0, tiled=True)

    image = apply_operator(beta_hat, ld_band, shifts, ridge_shift, halo)
    image_all = lax.all_gather(image, "ind", axis=0, tiled=True)
    image2 = apply_operator(image, ld_band, shifts, ridge_shift, halo)

    moments = jnp.stack(
        [
            jnp.sum(beta_hat * beta_hat, axis=1),
            jnp.sum(beta_hat * image, axis=1),
            jnp.sum(image * image, axis=1),
            jnp.sum(image * image2, axis=1),
        ]
    )
    placed = jnp.zeros((4, traits), jnp.float32)
    placed = lax.dynamic_update_slice_in_dim(placed, moments, me_ind * traits_here, 1)
    m0, m1, m2, m3 = all_sum(placed, ("ind", "snp"), n_all)

    alpha1 = m0 / m1
    norm1 = alpha1 * alpha1 * m2 - m0
    ratio = norm1 / m0
    grow = 1.0 + ratio
    curv = grow * grow * m1 - 2.0 * grow * alpha1 * m2 + alpha1 * alpha1 * m3
    alpha2 = norm1 / curv
    residual = beta_all - alpha1[:, None] * image_all
    direction = residual + ratio[:, None] * beta_all
    weights_all = alpha1[:, None] * beta_all + alpha2[:, None] * direction
    weights = lax.dynamic_slice_in_dim(weights_all, me_ind * traits_here, traits_here, 0)

    rounded = weights_all.astype(jnp.bfloat16)
    partial = lax.dot_general(
        rounded, genotypes, (((1,), (1,)), ((), ())), preferred_element_type=jnp.float32
    )
    mean_part = jnp.sum(rounded.astype(jnp.float32) * colsum[None, :], axis=1)
    inds_here = genotypes.shape[0]
    share = inds_here // n_snp
    chunks = partial.reshape(traits, n_snp, share).transpose(1, 0, 2).reshape(n_snp, traits * share)
    extra = jnp.broadcast_to(jnp.pad(mean_part, (0, 128 - traits % 128 if traits % 128 else 0))[None], (n_snp, -(-traits // 128) * 128))
    sent = jnp.concatenate([chunks, extra], axis=1).reshape(n_snp, -1, 128)
    got = jnp.sum(lax.all_to_all(sent, "snp", 0, 0, tiled=True), axis=0).reshape(-1)
    complete = got[: traits * share].reshape(traits, share)
    count = inds_here * n_ind
    average = got[traits * share : traits * share + traits] / count
    centred = complete - average[:, None]
    variance = all_sum(jnp.sum(centred * centred, axis=1), ("ind", "snp"), n_all) / count
    scores = centred * lax.rsqrt(variance + 1e-05)[:, None]
    return (weights, scores)


def solution(mesh):
    placed = (P("ind", "snp"), P("snp", None), P("snp"), P("ind"), P("ind", "snp"))
    return jax.shard_map(
        local,
        mesh=mesh,
        in_specs=placed,
        out_specs=(P("ind", "snp"), P(None, ("ind", "snp"))),
        check_vma=False,
    )
```

```python
import jax
import jax.numpy as jnp
from jax import lax
from jax.sharding import PartitionSpec as P

BLK = 128
ITERS = 2
M_GENOME = 1100000
N_GWAS = 1000000
REACH = 416
SHIFT_BITS = 7


def all_sum(x, axes, count):
    sent = jnp.broadcast_to(x[None], (count,) + x.shape)
    return jnp.sum(lax.all_to_all(sent, axes, 0, 0, tiled=True), axis=0)


def windows_of(padded, shifts, band_cols, blocks_here):
    span = band_cols + (1 << SHIFT_BITS) - 1
    need = (blocks_here - 1) * BLK + span
    padded = jnp.pad(padded, ((0, 0), (0, max(0, need - padded.shape[1]))))
    wide = jnp.stack([padded[:, b * BLK : b * BLK + span] for b in range(blocks_here)])
    for bit in range(SHIFT_BITS):
        step = 1 << bit
        take = ((shifts >> bit) & 1)[:, None, None] == 1
        wide = jnp.where(take, wide[:, :, step:], wide[:, :, :-step])
    return wide[:, :, :band_cols]


def apply_operator(extended, vector, ld_band, shifts, ridge_shift):
    band_cols = ld_band.shape[1]
    blocks_here = ld_band.shape[0] // BLK
    windows = windows_of(extended, shifts, band_cols, blocks_here)
    blocks = ld_band.reshape(blocks_here, BLK, band_cols)
    product = jnp.einsum("btk,brk->tbr", windows, blocks, precision=lax.Precision.HIGHEST)
    return product.reshape(vector.shape) + ridge_shift[:, None] * vector


def spread_operator(vector, ld_band, shifts, ridge_shift, halo):
    band_cols = ld_band.shape[1]
    blocks_here = ld_band.shape[0] // BLK
    traits, rows = vector.shape
    span = band_cols + (1 << SHIFT_BITS) - 1
    blocks = ld_band.reshape(blocks_here, BLK, band_cols)
    pieces = jnp.einsum(
        "tbr,brk->btk", vector.reshape(traits, blocks_here, BLK), blocks,
        precision=lax.Precision.HIGHEST,
    )
    wide = jnp.pad(pieces, ((0, 0), (0, 0), (0, span - band_cols)))
    for bit in range(SHIFT_BITS):
        step = 1 << bit
        take = ((shifts >> bit) & 1)[:, None, None] == 1
        moved = jnp.pad(wide, ((0, 0), (0, 0), (step, 0)))[:, :, :span]
        wide = jnp.where(take, moved, wide)
    width = max((blocks_here - 1) * BLK + span, rows + 2 * halo)
    own = sum(
        jnp.pad(wide[b], ((0, 0), (b * BLK, width - b * BLK - span))) for b in range(blocks_here)
    )[:, : rows + 2 * halo]
    own = own + jnp.pad(ridge_shift[:, None] * vector, ((0, 0), (halo, halo)))
    count = lax.axis_size("snp")
    forward = [(i, i + 1) for i in range(count - 1)]
    backward = [(target, source) for source, target in forward]
    from_left = lax.ppermute(own[:, rows:], "snp", forward)
    from_right = lax.ppermute(own[:, : 2 * halo], "snp", backward)
    return own + jnp.pad(from_left, ((0, 0), (0, rows))) + jnp.pad(from_right, ((0, 0), (rows, 0)))


def local(beta_hat, ld_band, band_start, heritability, genotypes):
    n_snp = lax.axis_size("snp")
    n_ind = lax.axis_size("ind")
    n_all = n_snp * n_ind
    me_ind = lax.axis_index("ind")
    traits_here, rows_here = beta_hat.shape
    traits = traits_here * n_ind
    halo = ld_band.shape[1] - BLK - REACH
    offsets = band_start - lax.axis_index("snp") * rows_here + halo
    shifts = offsets - jnp.arange(band_start.shape[0], dtype=jnp.int32) * BLK

    ridge_shift = M_GENOME / N_GWAS / heritability
    colsum = jnp.sum(genotypes.astype(jnp.float32), axis=0)
    colsum = all_sum(colsum, "ind", n_ind)
    beta_all = lax.all_gather(beta_hat, "ind", axis=0, tiled=True)

    extended = spread_operator(beta_hat, ld_band, shifts, ridge_shift, halo)
    image = extended[:, halo : halo + rows_here]
    image_all = lax.all_gather(image, "ind", axis=0, tiled=True)
    image2 = apply_operator(extended, image, ld_band, shifts, ridge_shift)

    moments = jnp.stack(
        [
            jnp.sum(beta_hat * beta_hat, axis=1),
            jnp.sum(beta_hat * image, axis=1),
            jnp.sum(image * image, axis=1),
            jnp.sum(image * image2, axis=1),
        ]
    )
    placed = jnp.zeros((4, traits), jnp.float32)
    placed = lax.dynamic_update_slice_in_dim(placed, moments, me_ind * traits_here, 1)
    m0, m1, m2, m3 = all_sum(placed, ("ind", "snp"), n_all)

    alpha1 = m0 / m1
    norm1 = alpha1 * alpha1 * m2 - m0
    ratio = norm1 / m0
    grow = 1.0 + ratio
    curv = grow * grow * m1 - 2.0 * grow * alpha1 * m2 + alpha1 * alpha1 * m3
    alpha2 = norm1 / curv
    residual = beta_all - alpha1[:, None] * image_all
    direction = residual + ratio[:, None] * beta_all
    weights_all = alpha1[:, None] * beta_all + alpha2[:, None] * direction
    weights = lax.dynamic_slice_in_dim(weights_all, me_ind * traits_here, traits_here, 0)

    rounded = weights_all.astype(jnp.bfloat16)
    partial = lax.dot_general(
        rounded, genotypes, (((1,), (1,)), ((), ())), preferred_element_type=jnp.float32
    )
    mean_part = jnp.sum(rounded.astype(jnp.float32) * colsum[None, :], axis=1)
    inds_here = genotypes.shape[0]
    share = inds_here // n_snp
    chunks = partial.reshape(traits, n_snp, share).transpose(1, 0, 2).reshape(n_snp, traits * share)
    extra = jnp.broadcast_to(jnp.pad(mean_part, (0, 128 - traits % 128 if traits % 128 else 0))[None], (n_snp, -(-traits // 128) * 128))
    sent = jnp.concatenate([chunks, extra], axis=1).reshape(n_snp, -1, 128)
    got = jnp.sum(lax.all_to_all(sent, "snp", 0, 0, tiled=True), axis=0).reshape(-1)
    complete = got[: traits * share].reshape(traits, share)
    count = inds_here * n_ind
    average = got[traits * share : traits * share + traits] / count
    centred = complete - average[:, None]
    variance = all_sum(jnp.sum(centred * centred, axis=1), ("ind", "snp"), n_all) / count
    scores = centred * lax.rsqrt(variance + 1e-05)[:, None]
    return (weights, scores)


def solution(mesh):
    placed = (P("ind", "snp"), P("snp", None), P("snp"), P("ind"), P("ind", "snp"))
    return jax.shard_map(
        local,
        mesh=mesh,
        in_specs=placed,
        out_specs=(P("ind", "snp"), P(None, ("ind", "snp"))),
        check_vma=False,
    )
```

```python
import jax
import jax.numpy as jnp
from jax import lax
from jax.sharding import PartitionSpec as P

BLK = 128
ITERS = 2
M_GENOME = 1100000
N_GWAS = 1000000
REACH = 416
SHIFT_BITS = 7


def all_sum(x, axes, count):
    sent = jnp.broadcast_to(x[None], (count,) + x.shape)
    return jnp.sum(lax.all_to_all(sent, axes, 0, 0, tiled=True), axis=0)


def windows_of(padded, shifts, band_cols, blocks_here):
    span = band_cols + (1 << SHIFT_BITS) - 1
    need = (blocks_here - 1) * BLK + span
    padded = jnp.pad(padded, ((0, 0), (0, max(0, need - padded.shape[1]))))
    wide = jnp.stack([padded[:, b * BLK : b * BLK + span] for b in range(blocks_here)])
    for bit in range(SHIFT_BITS):
        step = 1 << bit
        take = ((shifts >> bit) & 1)[:, None, None] == 1
        wide = jnp.where(take, wide[:, :, step:], wide[:, :, :-step])
    return wide[:, :, :band_cols]


def apply_operator(extended, vector, ld_band, shifts, ridge_shift):
    band_cols = ld_band.shape[1]
    blocks_here = ld_band.shape[0] // BLK
    windows = windows_of(extended, shifts, band_cols, blocks_here)
    blocks = ld_band.reshape(blocks_here, BLK, band_cols)
    product = jnp.einsum("btk,brk->tbr", windows, blocks, precision=lax.Precision.HIGHEST)
    return product.reshape(vector.shape) + ridge_shift[:, None] * vector


def spread_operator(vector, ld_band, shifts, ridge_shift, halo):
    band_cols = ld_band.shape[1]
    blocks_here = ld_band.shape[0] // BLK
    traits, rows = vector.shape
    span = band_cols + (1 << SHIFT_BITS) - 1
    blocks = ld_band.reshape(blocks_here, BLK, band_cols)
    pieces = jnp.einsum(
        "tbr,brk->btk", vector.reshape(traits, blocks_here, BLK), blocks,
        precision=lax.Precision.HIGHEST,
    )
    wide = jnp.pad(pieces, ((0, 0), (0, 0), (0, span - band_cols)))
    for bit in range(SHIFT_BITS):
        step = 1 << bit
        take = ((shifts >> bit) & 1)[:, None, None] == 1
        moved = jnp.pad(wide, ((0, 0), (0, 0), (step, 0)))[:, :, :span]
        wide = jnp.where(take, moved, wide)
    width = max((blocks_here - 1) * BLK + span, rows + 2 * halo)
    own = sum(
        jnp.pad(wide[b], ((0, 0), (b * BLK, width - b * BLK - span))) for b in range(blocks_here)
    )[:, : rows + 2 * halo]
    own = own + jnp.pad(ridge_shift[:, None] * vector, ((0, 0), (halo, halo)))
    count = lax.axis_size("snp")
    forward = [(i, i + 1) for i in range(count - 1)]
    backward = [(target, source) for source, target in forward]
    from_left = lax.ppermute(own[:, rows:], "snp", forward)
    from_right = lax.ppermute(own[:, : 2 * halo], "snp", backward)
    return own + jnp.pad(from_left, ((0, 0), (0, rows))) + jnp.pad(from_right, ((0, 0), (rows, 0)))


def local(beta_hat, ld_band, band_start, heritability, genotypes):
    n_snp = lax.axis_size("snp")
    n_ind = lax.axis_size("ind")
    n_all = n_snp * n_ind
    traits_here, rows_here = beta_hat.shape
    traits = traits_here * n_ind
    halo = ld_band.shape[1] - BLK - REACH
    offsets = band_start - lax.axis_index("snp") * rows_here + halo
    shifts = offsets - jnp.arange(band_start.shape[0], dtype=jnp.int32) * BLK

    ridge_shift = M_GENOME / N_GWAS / heritability
    extended = spread_operator(beta_hat, ld_band, shifts, ridge_shift, halo)
    image = extended[:, halo : halo + rows_here]
    image2 = apply_operator(extended, image, ld_band, shifts, ridge_shift)

    moments = jnp.stack(
        [
            jnp.sum(beta_hat * beta_hat, axis=1),
            jnp.sum(beta_hat * image, axis=1),
            jnp.sum(image * image, axis=1),
            jnp.sum(image * image2, axis=1),
        ]
    )
    m0, m1, m2, m3 = all_sum(moments, "snp", n_snp)

    alpha1 = m0 / m1
    norm1 = alpha1 * alpha1 * m2 - m0
    ratio = norm1 / m0
    grow = 1.0 + ratio
    curv = grow * grow * m1 - 2.0 * grow * alpha1 * m2 + alpha1 * alpha1 * m3
    alpha2 = norm1 / curv
    residual = beta_hat - alpha1[:, None] * image
    direction = residual + ratio[:, None] * beta_hat
    weights = alpha1[:, None] * beta_hat + alpha2[:, None] * direction

    rounded = lax.all_gather(weights.astype(jnp.bfloat16), "ind", axis=0, tiled=True)
    partial = lax.dot_general(
        rounded, genotypes, (((1,), (1,)), ((), ())), preferred_element_type=jnp.float32
    )
    inds_here = genotypes.shape[0]
    share = inds_here // n_snp
    chunks = partial.reshape(traits, n_snp, share).transpose(1, 0, 2)
    complete = jnp.sum(lax.all_to_all(chunks, "snp", 0, 0, tiled=True), axis=0)
    count = inds_here * n_ind
    local_sum = jnp.sum(complete, axis=1)
    local_centred = complete - (local_sum / share)[:, None]
    local_square = jnp.sum(local_centred * local_centred, axis=1)
    both = jnp.stack([local_sum, local_square])
    sent = jnp.broadcast_to(both[None], (n_all,) + both.shape)
    every = lax.all_to_all(sent, ("ind", "snp"), 0, 0, tiled=True)
    average = jnp.sum(every[:, 0], axis=0) / count
    spread = every[:, 0] / share - average[None, :]
    squares = jnp.sum(every[:, 1], axis=0) + share * jnp.sum(spread * spread, axis=0)
    variance = squares / count
    centred = complete - average[:, None]
    scores = centred * lax.rsqrt(variance + 1e-05)[:, None]
    return (weights, scores)


def solution(mesh):
    placed = (P("ind", "snp"), P("snp", None), P("snp"), P("ind"), P("ind", "snp"))
    return jax.shard_map(
        local,
        mesh=mesh,
        in_specs=placed,
        out_specs=(P("ind", "snp"), P(None, ("ind", "snp"))),
        check_vma=False,
    )
```

```python
import jax
import jax.numpy as jnp
from jax import lax
from jax.sharding import PartitionSpec as P

BLK = 128
ITERS = 2
M_GENOME = 1100000
N_GWAS = 1000000
REACH = 416
SHIFT_BITS = 7


def all_sum(x, axes, count):
    sent = jnp.broadcast_to(x[None], (count,) + x.shape)
    return jnp.sum(lax.all_to_all(sent, axes, 0, 0, tiled=True), axis=0)


def windows_of(padded, shifts, band_cols, blocks_here):
    span = band_cols + (1 << SHIFT_BITS) - 1
    need = (blocks_here - 1) * BLK + span
    padded = jnp.pad(padded, ((0, 0), (0, max(0, need - padded.shape[1]))))
    wide = jnp.stack([padded[:, b * BLK : b * BLK + span] for b in range(blocks_here)])
    for bit in range(SHIFT_BITS):
        step = 1 << bit
        take = ((shifts >> bit) & 1)[:, None, None] == 1
        wide = jnp.where(take, wide[:, :, step:], wide[:, :, :-step])
    return wide[:, :, :band_cols]


def apply_operator(extended, vector, ld_band, shifts, ridge_shift):
    band_cols = ld_band.shape[1]
    blocks_here = ld_band.shape[0] // BLK
    windows = windows_of(extended, shifts, band_cols, blocks_here)
    blocks = ld_band.reshape(blocks_here, BLK, band_cols)
    product = jnp.einsum("btk,brk->tbr", windows, blocks, precision=lax.Precision.HIGHEST)
    return product.reshape(vector.shape) + ridge_shift[:, None] * vector


def spread_operator(vector, ld_band, shifts, ridge_shift, halo):
    band_cols = ld_band.shape[1]
    blocks_here = ld_band.shape[0] // BLK
    traits, rows = vector.shape
    span = band_cols + (1 << SHIFT_BITS) - 1
    blocks = ld_band.reshape(blocks_here, BLK, band_cols)
    pieces = jnp.einsum(
        "tbr,brk->btk", vector.reshape(traits, blocks_here, BLK), blocks,
        precision=lax.Precision.HIGHEST,
    )
    wide = jnp.pad(pieces, ((0, 0), (0, 0), (0, span - band_cols)))
    for bit in range(SHIFT_BITS):
        step = 1 << bit
        take = ((shifts >> bit) & 1)[:, None, None] == 1
        moved = jnp.pad(wide, ((0, 0), (0, 0), (step, 0)))[:, :, :span]
        wide = jnp.where(take, moved, wide)
    width = max((blocks_here - 1) * BLK + span, rows + 2 * halo)
    own = sum(
        jnp.pad(wide[b], ((0, 0), (b * BLK, width - b * BLK - span))) for b in range(blocks_here)
    )[:, : rows + 2 * halo]
    own = own + jnp.pad(ridge_shift[:, None] * vector, ((0, 0), (halo, halo)))
    count = lax.axis_size("snp")
    forward = [(i, i + 1) for i in range(count - 1)]
    backward = [(target, source) for source, target in forward]
    from_left = lax.ppermute(own[:, rows:], "snp", forward)
    from_right = lax.ppermute(own[:, : 2 * halo], "snp", backward)
    return own + jnp.pad(from_left, ((0, 0), (0, rows))) + jnp.pad(from_right, ((0, 0), (rows, 0)))


def local(beta_hat, ld_band, band_start, heritability, genotypes):
    n_snp = lax.axis_size("snp")
    n_ind = lax.axis_size("ind")
    n_all = n_snp * n_ind
    me_ind = lax.axis_index("ind")
    traits_here, rows_here = beta_hat.shape
    traits = traits_here * n_ind
    halo = ld_band.shape[1] - BLK - REACH
    offsets = band_start - lax.axis_index("snp") * rows_here + halo
    shifts = offsets - jnp.arange(band_start.shape[0], dtype=jnp.int32) * BLK

    ridge_shift = M_GENOME / N_GWAS / heritability
    extended = spread_operator(beta_hat, ld_band, shifts, ridge_shift, halo)
    image = extended[:, halo : halo + rows_here]
    pair = jnp.concatenate([beta_hat, image], axis=0)
    arrived = [pair] + [
        lax.ppermute(pair, "ind", [(j, (j + k) % n_ind) for j in range(n_ind)])
        for k in range(1, n_ind)
    ]
    image2 = apply_operator(extended, image, ld_band, shifts, ridge_shift)

    moments = jnp.stack(
        [
            jnp.sum(beta_hat * beta_hat, axis=1),
            jnp.sum(beta_hat * image, axis=1),
            jnp.sum(image * image, axis=1),
            jnp.sum(image * image2, axis=1),
        ]
    )
    placed = jnp.zeros((4, traits), jnp.float32)
    placed = lax.dynamic_update_slice_in_dim(placed, moments, me_ind * traits_here, 1)
    m0, m1, m2, m3 = all_sum(placed, ("ind", "snp"), n_all)
    slots = (me_ind - jnp.arange(n_ind)) % n_ind
    ordered = jnp.take(jnp.stack(arrived), slots, axis=0)
    beta_all = ordered[:, :traits_here].reshape(traits, rows_here)
    image_all = ordered[:, traits_here:].reshape(traits, rows_here)

    alpha1 = m0 / m1
    norm1 = alpha1 * alpha1 * m2 - m0
    ratio = norm1 / m0
    grow = 1.0 + ratio
    curv = grow * grow * m1 - 2.0 * grow * alpha1 * m2 + alpha1 * alpha1 * m3
    alpha2 = norm1 / curv
    residual = beta_all - alpha1[:, None] * image_all
    direction = residual + ratio[:, None] * beta_all
    weights_all = alpha1[:, None] * beta_all + alpha2[:, None] * direction
    weights = lax.dynamic_slice_in_dim(weights_all, me_ind * traits_here, traits_here, 0)

    rounded = weights_all.astype(jnp.bfloat16)
    partial = lax.dot_general(
        rounded, genotypes, (((1,), (1,)), ((), ())), preferred_element_type=jnp.float32
    )
    inds_here = genotypes.shape[0]
    share = inds_here // n_snp
    chunks = partial.reshape(traits, n_snp, share).transpose(1, 0, 2)
    complete = jnp.sum(lax.all_to_all(chunks, "snp", 0, 0, tiled=True), axis=0)
    count = inds_here * n_ind
    local_sum = jnp.sum(complete, axis=1)
    local_centred = complete - (local_sum / share)[:, None]
    local_square = jnp.sum(local_centred * local_centred, axis=1)
    both = jnp.stack([local_sum, local_square])
    sent = jnp.broadcast_to(both[None], (n_all,) + both.shape)
    every = lax.all_to_all(sent, ("ind", "snp"), 0, 0, tiled=True)
    average = jnp.sum(every[:, 0], axis=0) / count
    spread = every[:, 0] / share - average[None, :]
    squares = jnp.sum(every[:, 1], axis=0) + share * jnp.sum(spread * spread, axis=0)
    variance = squares / count
    centred = complete - average[:, None]
    scores = centred * lax.rsqrt(variance + 1e-05)[:, None]
    return (weights, scores)


def solution(mesh):
    placed = (P("ind", "snp"), P("snp", None), P("snp"), P("ind"), P("ind", "snp"))
    return jax.shard_map(
        local,
        mesh=mesh,
        in_specs=placed,
        out_specs=(P("ind", "snp"), P(None, ("ind", "snp"))),
        check_vma=False,
    )
```

```python
import jax
import jax.numpy as jnp
from jax import lax
from jax.sharding import PartitionSpec as P

BLK = 128
ITERS = 2
M_GENOME = 1100000
N_GWAS = 1000000
REACH = 416
SHIFT_BITS = 7


def all_sum(x, axes, count):
    sent = jnp.broadcast_to(x[None], (count,) + x.shape)
    return jnp.sum(lax.all_to_all(sent, axes, 0, 0, tiled=True), axis=0)


def windows_of(padded, shifts, band_cols, blocks_here):
    span = band_cols + (1 << SHIFT_BITS) - 1
    need = (blocks_here - 1) * BLK + span
    padded = jnp.pad(padded, ((0, 0), (0, max(0, need - padded.shape[1]))))
    wide = jnp.stack([padded[:, b * BLK : b * BLK + span] for b in range(blocks_here)])
    for bit in range(SHIFT_BITS):
        step = 1 << bit
        take = ((shifts >> bit) & 1)[:, None, None] == 1
        wide = jnp.where(take, wide[:, :, step:], wide[:, :, :-step])
    return wide[:, :, :band_cols]


def apply_operator(extended, vector, ld_band, shifts, ridge_shift):
    band_cols = ld_band.shape[1]
    blocks_here = ld_band.shape[0] // BLK
    windows = windows_of(extended, shifts, band_cols, blocks_here)
    blocks = ld_band.reshape(blocks_here, BLK, band_cols)
    product = jnp.einsum("btk,brk->tbr", windows, blocks, precision=lax.Precision.HIGH)
    return product.reshape(vector.shape) + ridge_shift[:, None] * vector


def spread_operator(vector, ld_band, shifts, ridge_shift, halo):
    band_cols = ld_band.shape[1]
    blocks_here = ld_band.shape[0] // BLK
    traits, rows = vector.shape
    span = band_cols + (1 << SHIFT_BITS) - 1
    blocks = ld_band.reshape(blocks_here, BLK, band_cols)
    pieces = jnp.einsum(
        "tbr,brk->btk", vector.reshape(traits, blocks_here, BLK), blocks,
        precision=lax.Precision.HIGH,
    )
    wide = jnp.pad(pieces, ((0, 0), (0, 0), (0, span - band_cols)))
    for bit in range(SHIFT_BITS):
        step = 1 << bit
        take = ((shifts >> bit) & 1)[:, None, None] == 1
        moved = jnp.pad(wide, ((0, 0), (0, 0), (step, 0)))[:, :, :span]
        wide = jnp.where(take, moved, wide)
    width = max((blocks_here - 1) * BLK + span, rows + 2 * halo)
    own = sum(
        jnp.pad(wide[b], ((0, 0), (b * BLK, width - b * BLK - span))) for b in range(blocks_here)
    )[:, : rows + 2 * halo]
    own = own + jnp.pad(ridge_shift[:, None] * vector, ((0, 0), (halo, halo)))
    count = lax.axis_size("snp")
    forward = [(i, i + 1) for i in range(count - 1)]
    backward = [(target, source) for source, target in forward]
    from_left = lax.ppermute(own[:, rows:], "snp", forward)
    from_right = lax.ppermute(own[:, : 2 * halo], "snp", backward)
    return own + jnp.pad(from_left, ((0, 0), (0, rows))) + jnp.pad(from_right, ((0, 0), (rows, 0)))


def local(beta_hat, ld_band, band_start, heritability, genotypes):
    n_snp = lax.axis_size("snp")
    n_ind = lax.axis_size("ind")
    n_all = n_snp * n_ind
    traits_here, rows_here = beta_hat.shape
    traits = traits_here * n_ind
    halo = ld_band.shape[1] - BLK - REACH
    offsets = band_start - lax.axis_index("snp") * rows_here + halo
    shifts = offsets - jnp.arange(band_start.shape[0], dtype=jnp.int32) * BLK

    ridge_shift = M_GENOME / N_GWAS / heritability
    extended = spread_operator(beta_hat, ld_band, shifts, ridge_shift, halo)
    image = extended[:, halo : halo + rows_here]
    image2 = apply_operator(extended, image, ld_band, shifts, ridge_shift)

    moments = jnp.stack(
        [
            jnp.sum(beta_hat * beta_hat, axis=1),
            jnp.sum(beta_hat * image, axis=1),
            jnp.sum(image * image, axis=1),
            jnp.sum(image * image2, axis=1),
        ]
    )
    m0, m1, m2, m3 = all_sum(moments, "snp", n_snp)

    alpha1 = m0 / m1
    norm1 = alpha1 * alpha1 * m2 - m0
    ratio = norm1 / m0
    grow = 1.0 + ratio
    curv = grow * grow * m1 - 2.0 * grow * alpha1 * m2 + alpha1 * alpha1 * m3
    alpha2 = norm1 / curv
    residual = beta_hat - alpha1[:, None] * image
    direction = residual + ratio[:, None] * beta_hat
    weights = alpha1[:, None] * beta_hat + alpha2[:, None] * direction

    rounded = lax.all_gather(weights.astype(jnp.bfloat16), "ind", axis=0, tiled=True)
    partial = lax.dot_general(
        rounded, genotypes, (((1,), (1,)), ((), ())), preferred_element_type=jnp.float32
    )
    inds_here = genotypes.shape[0]
    share = inds_here // n_snp
    chunks = partial.reshape(traits, n_snp, share).transpose(1, 0, 2)
    complete = jnp.sum(lax.all_to_all(chunks, "snp", 0, 0, tiled=True), axis=0)
    count = inds_here * n_ind
    local_sum = jnp.sum(complete, axis=1)
    local_centred = complete - (local_sum / share)[:, None]
    local_square = jnp.sum(local_centred * local_centred, axis=1)
    both = jnp.stack([local_sum, local_square])
    sent = jnp.broadcast_to(both[None], (n_all,) + both.shape)
    every = lax.all_to_all(sent, ("ind", "snp"), 0, 0, tiled=True)
    average = jnp.sum(every[:, 0], axis=0) / count
    spread = every[:, 0] / share - average[None, :]
    squares = jnp.sum(every[:, 1], axis=0) + share * jnp.sum(spread * spread, axis=0)
    variance = squares / count
    centred = complete - average[:, None]
    scores = centred * lax.rsqrt(variance + 1e-05)[:, None]
    return (weights, scores)


def solution(mesh):
    placed = (P("ind", "snp"), P("snp", None), P("snp"), P("ind"), P("ind", "snp"))
    return jax.shard_map(
        local,
        mesh=mesh,
        in_specs=placed,
        out_specs=(P("ind", "snp"), P(None, ("ind", "snp"))),
        check_vma=False,
    )
```

```python
import jax
import jax.numpy as jnp
from jax import lax
from jax.sharding import PartitionSpec as P

BLK = 128
ITERS = 2
M_GENOME = 1100000
N_GWAS = 1000000
REACH = 416
SHIFT_BITS = 7


def all_sum(x, axes, count):
    sent = jnp.broadcast_to(x[None], (count,) + x.shape)
    return jnp.sum(lax.all_to_all(sent, axes, 0, 0, tiled=True), axis=0)


def windows_of(padded, shifts, band_cols, blocks_here):
    span = band_cols + (1 << SHIFT_BITS) - 1
    need = (blocks_here - 1) * BLK + span
    padded = jnp.pad(padded, ((0, 0), (0, max(0, need - padded.shape[1]))))
    wide = jnp.stack([padded[:, b * BLK : b * BLK + span] for b in range(blocks_here)])
    for bit in range(SHIFT_BITS):
        step = 1 << bit
        take = ((shifts >> bit) & 1)[:, None, None] == 1
        wide = jnp.where(take, wide[:, :, step:], wide[:, :, :-step])
    return wide[:, :, :band_cols]


def apply_operator(extended, vector, ld_band, shifts, ridge_shift):
    band_cols = ld_band.shape[1]
    blocks_here = ld_band.shape[0] // BLK
    windows = windows_of(extended, shifts, band_cols, blocks_here)
    blocks = ld_band.reshape(blocks_here, BLK, band_cols)
    product = jnp.einsum("btk,brk->tbr", windows, blocks, precision=lax.Precision.HIGH)
    return product.reshape(vector.shape) + ridge_shift[:, None] * vector


def spread_operator(vector, ld_band, shifts, ridge_shift, halo):
    band_cols = ld_band.shape[1]
    blocks_here = ld_band.shape[0] // BLK
    traits, rows = vector.shape
    span = band_cols + (1 << SHIFT_BITS) - 1
    blocks = ld_band.reshape(blocks_here, BLK, band_cols)
    pieces = jnp.einsum(
        "tbr,brk->btk", vector.reshape(traits, blocks_here, BLK), blocks,
        precision=lax.Precision.HIGH,
    )
    wide = jnp.pad(pieces, ((0, 0), (0, 0), (0, span - band_cols)))
    for bit in range(SHIFT_BITS):
        step = 1 << bit
        take = ((shifts >> bit) & 1)[:, None, None] == 1
        moved = jnp.pad(wide, ((0, 0), (0, 0), (step, 0)))[:, :, :span]
        wide = jnp.where(take, moved, wide)
    width = max((blocks_here - 1) * BLK + span, rows + 2 * halo)
    own = sum(
        jnp.pad(wide[b], ((0, 0), (b * BLK, width - b * BLK - span))) for b in range(blocks_here)
    )[:, : rows + 2 * halo]
    own = own + jnp.pad(ridge_shift[:, None] * vector, ((0, 0), (halo, halo)))
    count = lax.axis_size("snp")
    forward = [(i, i + 1) for i in range(count - 1)]
    backward = [(target, source) for source, target in forward]
    from_left = lax.ppermute(own[:, rows:], "snp", forward)
    from_right = lax.ppermute(own[:, : 2 * halo], "snp", backward)
    return own + jnp.pad(from_left, ((0, 0), (0, rows))) + jnp.pad(from_right, ((0, 0), (rows, 0)))


def local(beta_hat, ld_band, band_start, heritability, genotypes):
    n_snp = lax.axis_size("snp")
    n_ind = lax.axis_size("ind")
    n_all = n_snp * n_ind
    me_ind = lax.axis_index("ind")
    traits_here, rows_here = beta_hat.shape
    traits = traits_here * n_ind
    halo = ld_band.shape[1] - BLK - REACH
    offsets = band_start - lax.axis_index("snp") * rows_here + halo
    shifts = offsets - jnp.arange(band_start.shape[0], dtype=jnp.int32) * BLK

    ridge_shift = M_GENOME / N_GWAS / heritability
    extended = spread_operator(beta_hat, ld_band, shifts, ridge_shift, halo)
    image = extended[:, halo : halo + rows_here]
    image2 = apply_operator(extended, image, ld_band, shifts, ridge_shift)

    moments = jnp.stack(
        [
            jnp.sum(beta_hat * beta_hat, axis=1),
            jnp.sum(beta_hat * image, axis=1),
            jnp.sum(image * image, axis=1),
            jnp.sum(image * image2, axis=1),
        ]
    )
    placed = jnp.zeros((4, traits), jnp.float32)
    placed = lax.dynamic_update_slice_in_dim(placed, moments, me_ind * traits_here, 1)
    m0, m1, m2, m3 = all_sum(placed, ("ind", "snp"), n_all)
    pair = lax.all_gather(jnp.stack([beta_hat, image]), "ind", axis=1, tiled=True)
    beta_all, image_all = pair[0], pair[1]

    alpha1 = m0 / m1
    norm1 = alpha1 * alpha1 * m2 - m0
    ratio = norm1 / m0
    grow = 1.0 + ratio
    curv = grow * grow * m1 - 2.0 * grow * alpha1 * m2 + alpha1 * alpha1 * m3
    alpha2 = norm1 / curv
    residual = beta_all - alpha1[:, None] * image_all
    direction = residual + ratio[:, None] * beta_all
    weights_all = alpha1[:, None] * beta_all + alpha2[:, None] * direction
    weights = lax.dynamic_slice_in_dim(weights_all, me_ind * traits_here, traits_here, 0)

    rounded = weights_all.astype(jnp.bfloat16)
    partial = lax.dot_general(
        rounded, genotypes, (((1,), (1,)), ((), ())), preferred_element_type=jnp.float32
    )
    inds_here = genotypes.shape[0]
    share = inds_here // n_snp
    chunks = partial.reshape(traits, n_snp, share).transpose(1, 0, 2)
    complete = jnp.sum(lax.all_to_all(chunks, "snp", 0, 0, tiled=True), axis=0)
    count = inds_here * n_ind
    local_sum = jnp.sum(complete, axis=1)
    local_centred = complete - (local_sum / share)[:, None]
    local_square = jnp.sum(local_centred * local_centred, axis=1)
    both = jnp.stack([local_sum, local_square])
    sent = jnp.broadcast_to(both[None], (n_all,) + both.shape)
    every = lax.all_to_all(sent, ("ind", "snp"), 0, 0, tiled=True)
    average = jnp.sum(every[:, 0], axis=0) / count
    spread = every[:, 0] / share - average[None, :]
    squares = jnp.sum(every[:, 1], axis=0) + share * jnp.sum(spread * spread, axis=0)
    variance = squares / count
    centred = complete - average[:, None]
    scores = centred * lax.rsqrt(variance + 1e-05)[:, None]
    return (weights, scores)


def solution(mesh):
    placed = (P("ind", "snp"), P("snp", None), P("snp"), P("ind"), P("ind", "snp"))
    return jax.shard_map(
        local,
        mesh=mesh,
        in_specs=placed,
        out_specs=(P("ind", "snp"), P(None, ("ind", "snp"))),
        check_vma=False,
    )
```

```python
import jax
import jax.numpy as jnp
from jax import lax
from jax.sharding import PartitionSpec as P

BLK = 128
ITERS = 2
M_GENOME = 1100000
N_GWAS = 1000000
REACH = 416
SHIFT_BITS = 7


def all_sum(x, axes, count):
    sent = jnp.broadcast_to(x[None], (count,) + x.shape)
    return jnp.sum(lax.all_to_all(sent, axes, 0, 0, tiled=True), axis=0)


def windows_of(padded, shifts, band_cols, blocks_here):
    span = band_cols + (1 << SHIFT_BITS) - 1
    need = (blocks_here - 1) * BLK + span
    padded = jnp.pad(padded, ((0, 0), (0, max(0, need - padded.shape[1]))))
    wide = jnp.stack([padded[:, b * BLK : b * BLK + span] for b in range(blocks_here)])
    for bit in range(SHIFT_BITS):
        step = 1 << bit
        take = ((shifts >> bit) & 1)[:, None, None] == 1
        wide = jnp.where(take, wide[:, :, step:], wide[:, :, :-step])
    return wide[:, :, :band_cols]


def apply_operator(extended, vector, ld_band, shifts, ridge_shift):
    band_cols = ld_band.shape[1]
    blocks_here = ld_band.shape[0] // BLK
    windows = windows_of(extended, shifts, band_cols, blocks_here)
    blocks = ld_band.reshape(blocks_here, BLK, band_cols)
    product = jnp.einsum("btk,brk->tbr", windows, blocks, precision=lax.Precision.HIGH)
    return product.reshape(vector.shape) + ridge_shift[:, None] * vector


def spread_operator(vector, ld_band, shifts, ridge_shift, halo):
    band_cols = ld_band.shape[1]
    blocks_here = ld_band.shape[0] // BLK
    traits, rows = vector.shape
    span = band_cols + (1 << SHIFT_BITS) - 1
    blocks = ld_band.reshape(blocks_here, BLK, band_cols)
    pieces = jnp.einsum(
        "tbr,brk->btk", vector.reshape(traits, blocks_here, BLK), blocks,
        precision=lax.Precision.HIGH,
    )
    wide = jnp.pad(pieces, ((0, 0), (0, 0), (0, span - band_cols)))
    for bit in range(SHIFT_BITS):
        step = 1 << bit
        take = ((shifts >> bit) & 1)[:, None, None] == 1
        moved = jnp.pad(wide, ((0, 0), (0, 0), (step, 0)))[:, :, :span]
        wide = jnp.where(take, moved, wide)
    width = max((blocks_here - 1) * BLK + span, rows + 2 * halo)
    own = sum(
        jnp.pad(wide[b], ((0, 0), (b * BLK, width - b * BLK - span))) for b in range(blocks_here)
    )[:, : rows + 2 * halo]
    own = own + jnp.pad(ridge_shift[:, None] * vector, ((0, 0), (halo, halo)))
    count = lax.axis_size("snp")
    forward = [(i, i + 1) for i in range(count - 1)]
    backward = [(target, source) for source, target in forward]
    from_left = lax.ppermute(own[:, rows:], "snp", forward)
    from_right = lax.ppermute(own[:, : 2 * halo], "snp", backward)
    return own + jnp.pad(from_left, ((0, 0), (0, rows))) + jnp.pad(from_right, ((0, 0), (rows, 0)))


def local(beta_hat, ld_band, band_start, heritability, genotypes):
    n_snp = lax.axis_size("snp")
    n_ind = lax.axis_size("ind")
    n_all = n_snp * n_ind
    me_ind = lax.axis_index("ind")
    traits_here, rows_here = beta_hat.shape
    traits = traits_here * n_ind
    halo = ld_band.shape[1] - BLK - REACH
    offsets = band_start - lax.axis_index("snp") * rows_here + halo
    shifts = offsets - jnp.arange(band_start.shape[0], dtype=jnp.int32) * BLK

    ridge_shift = M_GENOME / N_GWAS / heritability
    extended = spread_operator(beta_hat, ld_band, shifts, ridge_shift, halo)
    image = extended[:, halo : halo + rows_here]
    image2 = apply_operator(extended, image, ld_band, shifts, ridge_shift)

    moments = jnp.stack(
        [
            jnp.sum(beta_hat * beta_hat, axis=1),
            jnp.sum(beta_hat * image, axis=1),
            jnp.sum(image * image, axis=1),
            jnp.sum(image * image2, axis=1),
        ]
    )
    placed = jnp.zeros((4, traits), jnp.float32)
    placed = lax.dynamic_update_slice_in_dim(placed, moments, me_ind * traits_here, 1)
    m0, m1, m2, m3 = all_sum(placed, ("ind", "snp"), n_all)
    pair = lax.all_gather(jnp.stack([beta_hat, image]), "ind", axis=1, tiled=True)
    beta_all, image_all = pair[0], pair[1]

    alpha1 = m0 / m1
    norm1 = alpha1 * alpha1 * m2 - m0
    ratio = norm1 / m0
    grow = 1.0 + ratio
    curv = grow * grow * m1 - 2.0 * grow * alpha1 * m2 + alpha1 * alpha1 * m3
    alpha2 = norm1 / curv
    residual = beta_all - alpha1[:, None] * image_all
    direction = residual + ratio[:, None] * beta_all
    weights_all = alpha1[:, None] * beta_all + alpha2[:, None] * direction
    weights = lax.dynamic_slice_in_dim(weights_all, me_ind * traits_here, traits_here, 0)

    rounded = weights_all.astype(jnp.bfloat16)
    partial = lax.dot_general(
        rounded, genotypes, (((1,), (1,)), ((), ())), preferred_element_type=jnp.float32
    )
    inds_here = genotypes.shape[0]
    share = inds_here // n_snp
    chunks = partial.reshape(traits, n_snp, share).transpose(1, 0, 2)
    weights, chunks = lax.optimization_barrier((weights, chunks))
    complete = jnp.sum(lax.all_to_all(chunks, "snp", 0, 0, tiled=True), axis=0)
    count = inds_here * n_ind
    local_sum = jnp.sum(complete, axis=1)
    local_centred = complete - (local_sum / share)[:, None]
    local_square = jnp.sum(local_centred * local_centred, axis=1)
    both = jnp.stack([local_sum, local_square])
    sent = jnp.broadcast_to(both[None], (n_all,) + both.shape)
    every = lax.all_to_all(sent, ("ind", "snp"), 0, 0, tiled=True)
    average = jnp.sum(every[:, 0], axis=0) / count
    spread = every[:, 0] / share - average[None, :]
    squares = jnp.sum(every[:, 1], axis=0) + share * jnp.sum(spread * spread, axis=0)
    variance = squares / count
    centred = complete - average[:, None]
    scores = centred * lax.rsqrt(variance + 1e-05)[:, None]
    return (weights, scores)


def solution(mesh):
    placed = (P("ind", "snp"), P("snp", None), P("snp"), P("ind"), P("ind", "snp"))
    return jax.shard_map(
        local,
        mesh=mesh,
        in_specs=placed,
        out_specs=(P("ind", "snp"), P(None, ("ind", "snp"))),
        check_vma=False,
    )
```

```python
import jax
import jax.numpy as jnp
from jax import lax
from jax.sharding import PartitionSpec as P

BLK = 128
ITERS = 2
M_GENOME = 1100000
N_GWAS = 1000000
REACH = 416
SHIFT_BITS = 7


def all_sum(x, axes, count):
    sent = jnp.broadcast_to(x[None], (count,) + x.shape)
    return jnp.sum(lax.all_to_all(sent, axes, 0, 0, tiled=True), axis=0)


def halves(x):
    high = x.astype(jnp.bfloat16)
    return high, (x - high.astype(jnp.float32)).astype(jnp.bfloat16)


def three_pass(spec, left, right):
    def dot(a, b):
        return jnp.einsum(spec, a, b, preferred_element_type=jnp.float32)
    return dot(left[0], right[0]) + (dot(left[0], right[1]) + dot(left[1], right[0]))


def windows_of(padded, shifts, band_cols, blocks_here):
    span = band_cols + (1 << SHIFT_BITS) - 1
    need = (blocks_here - 1) * BLK + span
    padded = jnp.pad(padded, ((0, 0), (0, max(0, need - padded.shape[1]))))
    wide = jnp.stack([padded[:, b * BLK : b * BLK + span] for b in range(blocks_here)])
    for bit in range(SHIFT_BITS):
        step = 1 << bit
        take = ((shifts >> bit) & 1)[:, None, None] == 1
        wide = jnp.where(take, wide[:, :, step:], wide[:, :, :-step])
    return wide[:, :, :band_cols]


def apply_operator(extended, vector, ld_band, shifts, ridge_shift):
    blocks_here, _, band_cols = ld_band[0].shape
    windows = windows_of(extended, shifts, band_cols, blocks_here)
    product = three_pass("btk,brk->tbr", halves(windows), ld_band)
    return product.reshape(vector.shape) + ridge_shift[:, None] * vector


def spread_operator(vector, ld_band, shifts, ridge_shift, halo):
    blocks_here, _, band_cols = ld_band[0].shape
    traits, rows = vector.shape
    span = band_cols + (1 << SHIFT_BITS) - 1
    pieces = three_pass("tbr,brk->btk", halves(vector.reshape(traits, blocks_here, BLK)), ld_band)
    wide = jnp.pad(pieces, ((0, 0), (0, 0), (0, span - band_cols)))
    for bit in range(SHIFT_BITS):
        step = 1 << bit
        take = ((shifts >> bit) & 1)[:, None, None] == 1
        moved = jnp.pad(wide, ((0, 0), (0, 0), (step, 0)))[:, :, :span]
        wide = jnp.where(take, moved, wide)
    width = max((blocks_here - 1) * BLK + span, rows + 2 * halo)
    own = sum(
        jnp.pad(wide[b], ((0, 0), (b * BLK, width - b * BLK - span))) for b in range(blocks_here)
    )[:, : rows + 2 * halo]
    own = own + jnp.pad(ridge_shift[:, None] * vector, ((0, 0), (halo, halo)))
    count = lax.axis_size("snp")
    forward = [(i, i + 1) for i in range(count - 1)]
    backward = [(target, source) for source, target in forward]
    from_left = lax.ppermute(own[:, rows:], "snp", forward)
    from_right = lax.ppermute(own[:, : 2 * halo], "snp", backward)
    return own + jnp.pad(from_left, ((0, 0), (0, rows))) + jnp.pad(from_right, ((0, 0), (rows, 0)))


def local(beta_hat, ld_band, band_start, heritability, genotypes):
    n_snp = lax.axis_size("snp")
    n_ind = lax.axis_size("ind")
    n_all = n_snp * n_ind
    traits_here, rows_here = beta_hat.shape
    traits = traits_here * n_ind
    halo = ld_band.shape[1] - BLK - REACH
    offsets = band_start - lax.axis_index("snp") * rows_here + halo
    shifts = offsets - jnp.arange(band_start.shape[0], dtype=jnp.int32) * BLK

    ridge_shift = M_GENOME / N_GWAS / heritability
    band_parts = halves(ld_band.reshape(-1, BLK, ld_band.shape[1]))
    extended = spread_operator(beta_hat, band_parts, shifts, ridge_shift, halo)
    image = extended[:, halo : halo + rows_here]
    image2 = apply_operator(extended, image, band_parts, shifts, ridge_shift)

    moments = jnp.stack(
        [
            jnp.sum(beta_hat * beta_hat, axis=1),
            jnp.sum(beta_hat * image, axis=1),
            jnp.sum(image * image, axis=1),
            jnp.sum(image * image2, axis=1),
        ]
    )
    m0, m1, m2, m3 = all_sum(moments, "snp", n_snp)

    alpha1 = m0 / m1
    norm1 = alpha1 * alpha1 * m2 - m0
    ratio = norm1 / m0
    grow = 1.0 + ratio
    curv = grow * grow * m1 - 2.0 * grow * alpha1 * m2 + alpha1 * alpha1 * m3
    alpha2 = norm1 / curv
    residual = beta_hat - alpha1[:, None] * image
    direction = residual + ratio[:, None] * beta_hat
    weights = alpha1[:, None] * beta_hat + alpha2[:, None] * direction

    rounded = lax.all_gather(weights.astype(jnp.bfloat16), "ind", axis=0, tiled=True)
    partial = lax.dot_general(
        rounded, genotypes, (((1,), (1,)), ((), ())), preferred_element_type=jnp.float32
    )
    inds_here = genotypes.shape[0]
    share = inds_here // n_snp
    chunks = partial.reshape(traits, n_snp, share).transpose(1, 0, 2)
    complete = jnp.sum(lax.all_to_all(chunks, "snp", 0, 0, tiled=True), axis=0)
    count = inds_here * n_ind
    local_sum = jnp.sum(complete, axis=1)
    local_centred = complete - (local_sum / share)[:, None]
    local_square = jnp.sum(local_centred * local_centred, axis=1)
    both = jnp.stack([local_sum, local_square])
    sent = jnp.broadcast_to(both[None], (n_all,) + both.shape)
    every = lax.all_to_all(sent, ("ind", "snp"), 0, 0, tiled=True)
    average = jnp.sum(every[:, 0], axis=0) / count
    spread = every[:, 0] / share - average[None, :]
    squares = jnp.sum(every[:, 1], axis=0) + share * jnp.sum(spread * spread, axis=0)
    variance = squares / count
    centred = complete - average[:, None]
    scores = centred * lax.rsqrt(variance + 1e-05)[:, None]
    return (weights, scores)


def solution(mesh):
    placed = (P("ind", "snp"), P("snp", None), P("snp"), P("ind"), P("ind", "snp"))
    return jax.shard_map(
        local,
        mesh=mesh,
        in_specs=placed,
        out_specs=(P("ind", "snp"), P(None, ("ind", "snp"))),
        check_vma=False,
    )
```

```python
import jax
import jax.numpy as jnp
from jax import lax
from jax.sharding import PartitionSpec as P

BLK = 128
ITERS = 2
M_GENOME = 1100000
N_GWAS = 1000000
REACH = 416
COARSE = 8
FINE = 8


def all_sum(x, axes, count):
    sent = jnp.broadcast_to(x[None], (count,) + x.shape)
    return jnp.sum(lax.all_to_all(sent, axes, 0, 0, tiled=True), axis=0)


def pick(source, choice, starts, length):
    out = source[:, :, starts[0] : starts[0] + length]
    for j in range(1, len(starts)):
        out = jnp.where(choice == j, source[:, :, starts[j] : starts[j] + length], out)
    return out


def windows_of(padded, shifts, band_cols, blocks_here):
    span = band_cols + COARSE * (FINE + 1) - 1
    need = (blocks_here - 1) * BLK + span
    padded = jnp.pad(padded, ((0, 0), (0, max(0, need - padded.shape[1]))))
    wide = jnp.stack([padded[:, b * BLK : b * BLK + span] for b in range(blocks_here)])
    coarse = (shifts // COARSE)[:, None, None]
    fine = (shifts % COARSE)[:, None, None]
    wide = pick(wide, coarse, [COARSE * j for j in range(FINE + 1)], band_cols + COARSE - 1)
    return pick(wide, fine, list(range(COARSE)), band_cols)


def apply_operator(extended, vector, ld_band, shifts, ridge_shift):
    band_cols = ld_band.shape[1]
    blocks_here = ld_band.shape[0] // BLK
    windows = windows_of(extended, shifts, band_cols, blocks_here)
    blocks = ld_band.reshape(blocks_here, BLK, band_cols)
    product = jnp.einsum("btk,brk->tbr", windows, blocks, precision=lax.Precision.HIGH)
    return product.reshape(vector.shape) + ridge_shift[:, None] * vector


def spread_operator(vector, ld_band, shifts, ridge_shift, halo):
    band_cols = ld_band.shape[1]
    blocks_here = ld_band.shape[0] // BLK
    traits, rows = vector.shape
    span = band_cols + COARSE * (FINE + 1) - 1
    blocks = ld_band.reshape(blocks_here, BLK, band_cols)
    pieces = jnp.einsum(
        "tbr,brk->btk", vector.reshape(traits, blocks_here, BLK), blocks,
        precision=lax.Precision.HIGH,
    )
    lead = COARSE * FINE + COARSE - 1
    source = jnp.pad(pieces, ((0, 0), (0, 0), (lead, lead)))
    coarse = (shifts // COARSE)[:, None, None]
    fine = (shifts % COARSE)[:, None, None]
    moved = pick(source, coarse, [COARSE * (FINE - j) for j in range(FINE + 1)], span + COARSE - 1)
    wide = pick(moved, fine, [COARSE - 1 - j for j in range(COARSE)], span)
    width = max((blocks_here - 1) * BLK + span, rows + 2 * halo)
    own = sum(
        jnp.pad(wide[b], ((0, 0), (b * BLK, width - b * BLK - span))) for b in range(blocks_here)
    )[:, : rows + 2 * halo]
    own = own + jnp.pad(ridge_shift[:, None] * vector, ((0, 0), (halo, halo)))
    count = lax.axis_size("snp")
    forward = [(i, i + 1) for i in range(count - 1)]
    backward = [(target, source) for source, target in forward]
    from_left = lax.ppermute(own[:, rows:], "snp", forward)
    from_right = lax.ppermute(own[:, : 2 * halo], "snp", backward)
    return own + jnp.pad(from_left, ((0, 0), (0, rows))) + jnp.pad(from_right, ((0, 0), (rows, 0)))


def local(beta_hat, ld_band, band_start, heritability, genotypes):
    n_snp = lax.axis_size("snp")
    n_ind = lax.axis_size("ind")
    n_all = n_snp * n_ind
    traits_here, rows_here = beta_hat.shape
    traits = traits_here * n_ind
    halo = ld_band.shape[1] - BLK - REACH
    offsets = band_start - lax.axis_index("snp") * rows_here + halo
    shifts = offsets - jnp.arange(band_start.shape[0], dtype=jnp.int32) * BLK

    ridge_shift = M_GENOME / N_GWAS / heritability
    extended = spread_operator(beta_hat, ld_band, shifts, ridge_shift, halo)
    image = extended[:, halo : halo + rows_here]
    image2 = apply_operator(extended, image, ld_band, shifts, ridge_shift)

    moments = jnp.stack(
        [
            jnp.sum(beta_hat * beta_hat, axis=1),
            jnp.sum(beta_hat * image, axis=1),
            jnp.sum(image * image, axis=1),
            jnp.sum(image * image2, axis=1),
        ]
    )
    m0, m1, m2, m3 = all_sum(moments, "snp", n_snp)

    alpha1 = m0 / m1
    norm1 = alpha1 * alpha1 * m2 - m0
    ratio = norm1 / m0
    grow = 1.0 + ratio
    curv = grow * grow * m1 - 2.0 * grow * alpha1 * m2 + alpha1 * alpha1 * m3
    alpha2 = norm1 / curv
    residual = beta_hat - alpha1[:, None] * image
    direction = residual + ratio[:, None] * beta_hat
    weights = alpha1[:, None] * beta_hat + alpha2[:, None] * direction

    rounded = lax.all_gather(weights.astype(jnp.bfloat16), "ind", axis=0, tiled=True)
    partial = lax.dot_general(
        rounded, genotypes, (((1,), (1,)), ((), ())), preferred_element_type=jnp.float32
    )
    inds_here = genotypes.shape[0]
    share = inds_here // n_snp
    chunks = partial.reshape(traits, n_snp, share).transpose(1, 0, 2)
    complete = jnp.sum(lax.all_to_all(chunks, "snp", 0, 0, tiled=True), axis=0)
    count = inds_here * n_ind
    local_sum = jnp.sum(complete, axis=1)
    local_centred = complete - (local_sum / share)[:, None]
    local_square = jnp.sum(local_centred * local_centred, axis=1)
    both = jnp.stack([local_sum, local_square])
    sent = jnp.broadcast_to(both[None], (n_all,) + both.shape)
    every = lax.all_to_all(sent, ("ind", "snp"), 0, 0, tiled=True)
    average = jnp.sum(every[:, 0], axis=0) / count
    spread = every[:, 0] / share - average[None, :]
    squares = jnp.sum(every[:, 1], axis=0) + share * jnp.sum(spread * spread, axis=0)
    variance = squares / count
    centred = complete - average[:, None]
    scores = centred * lax.rsqrt(variance + 1e-05)[:, None]
    return (weights, scores)


def solution(mesh):
    placed = (P("ind", "snp"), P("snp", None), P("snp"), P("ind"), P("ind", "snp"))
    return jax.shard_map(
        local,
        mesh=mesh,
        in_specs=placed,
        out_specs=(P("ind", "snp"), P(None, ("ind", "snp"))),
        check_vma=False,
    )
```

```python
import jax
import jax.numpy as jnp
from jax import lax
from jax.sharding import PartitionSpec as P

BLK = 128
ITERS = 2
M_GENOME = 1100000
N_GWAS = 1000000
REACH = 416
SHIFT_BITS = 7


def all_sum(x, axes, count):
    sent = jnp.broadcast_to(x[None], (count,) + x.shape)
    return jnp.sum(lax.all_to_all(sent, axes, 0, 0, tiled=True), axis=0)


def windows_of(padded, shifts, band_cols, blocks_here):
    span = band_cols + (1 << SHIFT_BITS) - 1
    need = (blocks_here - 1) * BLK + span
    padded = jnp.pad(padded, ((0, 0), (0, max(0, need - padded.shape[1]))))
    wide = jnp.stack([padded[:, b * BLK : b * BLK + span] for b in range(blocks_here)])
    for bit in range(SHIFT_BITS):
        step = 1 << bit
        take = ((shifts >> bit) & 1)[:, None, None] == 1
        wide = jnp.where(take, wide[:, :, step:], wide[:, :, :-step])
    return wide[:, :, :band_cols]


def apply_operator(extended, vector, ld_band, shifts, ridge_shift):
    band_cols = ld_band.shape[1]
    blocks_here = ld_band.shape[0] // BLK
    windows = windows_of(extended, shifts, band_cols, blocks_here)
    blocks = ld_band.reshape(blocks_here, BLK, band_cols)
    product = jnp.einsum("btk,brk->tbr", windows, blocks, precision=lax.Precision.HIGH)
    return product.reshape(vector.shape) + ridge_shift[:, None] * vector


def spread_operator(vector, ld_band, shifts, ridge_shift, halo):
    band_cols = ld_band.shape[1]
    blocks_here = ld_band.shape[0] // BLK
    traits, rows = vector.shape
    span = band_cols + (1 << SHIFT_BITS) - 1
    blocks = ld_band.reshape(blocks_here, BLK, band_cols)
    pieces = jnp.einsum(
        "tbr,brk->tbk", vector.reshape(traits, blocks_here, BLK), blocks,
        precision=lax.Precision.HIGH,
    )
    wide = jnp.pad(pieces, ((0, 0), (0, 0), (0, span - band_cols)))
    for bit in range(SHIFT_BITS):
        step = 1 << bit
        take = ((shifts >> bit) & 1)[None, :, None] == 1
        moved = jnp.pad(wide, ((0, 0), (0, 0), (step, 0)))[:, :, :span]
        wide = jnp.where(take, moved, wide)
    width = max((blocks_here - 1) * BLK + span, rows + 2 * halo)
    own = sum(
        jnp.pad(wide[:, b], ((0, 0), (b * BLK, width - b * BLK - span))) for b in range(blocks_here)
    )[:, : rows + 2 * halo]
    own = own + jnp.pad(ridge_shift[:, None] * vector, ((0, 0), (halo, halo)))
    count = lax.axis_size("snp")
    forward = [(i, i + 1) for i in range(count - 1)]
    backward = [(target, source) for source, target in forward]
    from_left = lax.ppermute(own[:, rows:], "snp", forward)
    from_right = lax.ppermute(own[:, : 2 * halo], "snp", backward)
    return own + jnp.pad(from_left, ((0, 0), (0, rows))) + jnp.pad(from_right, ((0, 0), (rows, 0)))


def local(beta_hat, ld_band, band_start, heritability, genotypes):
    n_snp = lax.axis_size("snp")
    n_ind = lax.axis_size("ind")
    n_all = n_snp * n_ind
    traits_here, rows_here = beta_hat.shape
    traits = traits_here * n_ind
    halo = ld_band.shape[1] - BLK - REACH
    offsets = band_start - lax.axis_index("snp") * rows_here + halo
    shifts = offsets - jnp.arange(band_start.shape[0], dtype=jnp.int32) * BLK

    ridge_shift = M_GENOME / N_GWAS / heritability
    extended = spread_operator(beta_hat, ld_band, shifts, ridge_shift, halo)
    image = extended[:, halo : halo + rows_here]
    image2 = apply_operator(extended, image, ld_band, shifts, ridge_shift)

    moments = jnp.stack(
        [
            jnp.sum(beta_hat * beta_hat, axis=1),
            jnp.sum(beta_hat * image, axis=1),
            jnp.sum(image * image, axis=1),
            jnp.sum(image * image2, axis=1),
        ]
    )
    m0, m1, m2, m3 = all_sum(moments, "snp", n_snp)

    alpha1 = m0 / m1
    norm1 = alpha1 * alpha1 * m2 - m0
    ratio = norm1 / m0
    grow = 1.0 + ratio
    curv = grow * grow * m1 - 2.0 * grow * alpha1 * m2 + alpha1 * alpha1 * m3
    alpha2 = norm1 / curv
    residual = beta_hat - alpha1[:, None] * image
    direction = residual + ratio[:, None] * beta_hat
    weights = alpha1[:, None] * beta_hat + alpha2[:, None] * direction

    rounded = lax.all_gather(weights.astype(jnp.bfloat16), "ind", axis=0, tiled=True)
    partial = lax.dot_general(
        rounded, genotypes, (((1,), (1,)), ((), ())), preferred_element_type=jnp.float32
    )
    inds_here = genotypes.shape[0]
    share = inds_here // n_snp
    chunks = partial.reshape(traits, n_snp, share).transpose(1, 0, 2)
    complete = jnp.sum(lax.all_to_all(chunks, "snp", 0, 0, tiled=True), axis=0)
    count = inds_here * n_ind
    local_sum = jnp.sum(complete, axis=1)
    local_centred = complete - (local_sum / share)[:, None]
    local_square = jnp.sum(local_centred * local_centred, axis=1)
    both = jnp.stack([local_sum, local_square])
    sent = jnp.broadcast_to(both[None], (n_all,) + both.shape)
    every = lax.all_to_all(sent, ("ind", "snp"), 0, 0, tiled=True)
    average = jnp.sum(every[:, 0], axis=0) / count
    spread = every[:, 0] / share - average[None, :]
    squares = jnp.sum(every[:, 1], axis=0) + share * jnp.sum(spread * spread, axis=0)
    variance = squares / count
    centred = complete - average[:, None]
    scores = centred * lax.rsqrt(variance + 1e-05)[:, None]
    return (weights, scores)


def solution(mesh):
    placed = (P("ind", "snp"), P("snp", None), P("snp"), P("ind"), P("ind", "snp"))
    return jax.shard_map(
        local,
        mesh=mesh,
        in_specs=placed,
        out_specs=(P("ind", "snp"), P(None, ("ind", "snp"))),
        check_vma=False,
    )
```

```python
import jax
import jax.numpy as jnp
from jax import lax
from jax.sharding import PartitionSpec as P

BLK = 128
ITERS = 2
M_GENOME = 1100000
N_GWAS = 1000000
REACH = 416
SHIFT_BITS = 7


def all_sum(x, axes, count):
    sent = jnp.broadcast_to(x[None], (count,) + x.shape)
    return jnp.sum(lax.all_to_all(sent, axes, 0, 0, tiled=True), axis=0)


def windows_of(padded, shifts, band_cols, blocks_here):
    span = band_cols + (1 << SHIFT_BITS) - 1
    need = (blocks_here - 1) * BLK + span
    padded = jnp.pad(padded, ((0, 0), (0, max(0, need - padded.shape[1]))))
    wide = jnp.stack([padded[:, b * BLK : b * BLK + span] for b in range(blocks_here)])
    for bit in range(SHIFT_BITS):
        step = 1 << bit
        take = ((shifts >> bit) & 1)[:, None, None] == 1
        wide = jnp.where(take, wide[:, :, step:], wide[:, :, :-step])
    return wide[:, :, :band_cols]


def apply_operator(extended, vector, ld_band, shifts, ridge_shift):
    band_cols = ld_band.shape[1]
    blocks_here = ld_band.shape[0] // BLK
    windows = windows_of(extended, shifts, band_cols, blocks_here)
    blocks = ld_band.reshape(blocks_here, BLK, band_cols)
    product = jnp.einsum("btk,brk->tbr", windows, blocks, precision=lax.Precision.HIGH)
    return product.reshape(vector.shape) + ridge_shift[:, None] * vector


def spread_operator(vector, ld_band, shifts, ridge_shift, halo):
    band_cols = ld_band.shape[1]
    blocks_here = ld_band.shape[0] // BLK
    traits, rows = vector.shape
    span = band_cols + (1 << SHIFT_BITS) - 1
    blocks = ld_band.reshape(blocks_here, BLK, band_cols)
    pieces = jnp.einsum(
        "tbr,brk->btk", vector.reshape(traits, blocks_here, BLK), blocks,
        precision=lax.Precision.HIGH,
    )
    wide = jnp.pad(pieces, ((0, 0), (0, 0), (0, span - band_cols)))
    for bit in range(SHIFT_BITS):
        step = 1 << bit
        take = ((shifts >> bit) & 1)[:, None, None] == 1
        moved = jnp.pad(wide, ((0, 0), (0, 0), (step, 0)))[:, :, :span]
        wide = jnp.where(take, moved, wide)
    width = max((blocks_here - 1) * BLK + span, rows + 2 * halo)
    own = sum(
        jnp.pad(wide[b], ((0, 0), (b * BLK, width - b * BLK - span))) for b in range(blocks_here)
    )[:, : rows + 2 * halo]
    own = own + jnp.pad(ridge_shift[:, None] * vector, ((0, 0), (halo, halo)))
    count = lax.axis_size("snp")
    forward = [(i, i + 1) for i in range(count - 1)]
    backward = [(target, source) for source, target in forward]
    from_left = lax.ppermute(own[:, rows:], "snp", forward)
    from_right = lax.ppermute(own[:, : 2 * halo], "snp", backward)
    return own + jnp.pad(from_left, ((0, 0), (0, rows))) + jnp.pad(from_right, ((0, 0), (rows, 0)))


def local(beta_hat, ld_band, band_start, heritability, genotypes):
    n_snp = lax.axis_size("snp")
    n_ind = lax.axis_size("ind")
    n_all = n_snp * n_ind
    me_ind = lax.axis_index("ind")
    traits_here, rows_here = beta_hat.shape
    traits = traits_here * n_ind
    halo = ld_band.shape[1] - BLK - REACH
    offsets = band_start - lax.axis_index("snp") * rows_here + halo
    shifts = offsets - jnp.arange(band_start.shape[0], dtype=jnp.int32) * BLK

    ridge_shift = M_GENOME / N_GWAS / heritability
    extended = spread_operator(beta_hat, ld_band, shifts, ridge_shift, halo)
    image = extended[:, halo : halo + rows_here]
    image2 = apply_operator(extended, image, ld_band, shifts, ridge_shift)

    moments = jnp.stack(
        [
            jnp.sum(beta_hat * beta_hat, axis=1),
            jnp.sum(beta_hat * image, axis=1),
            jnp.sum(image * image, axis=1),
            jnp.sum(image * image2, axis=1),
        ]
    )
    placed = jnp.zeros((4, traits), jnp.float32)
    placed = lax.dynamic_update_slice_in_dim(placed, moments, me_ind * traits_here, 1)
    m0, m1, m2, m3 = all_sum(placed, ("ind", "snp"), n_all)
    pair = lax.all_gather(jnp.stack([beta_hat, image]), "ind", axis=1, tiled=True)
    beta_all, image_all = pair[0], pair[1]

    alpha1 = m0 / m1
    norm1 = alpha1 * alpha1 * m2 - m0
    ratio = norm1 / m0
    grow = 1.0 + ratio
    curv = grow * grow * m1 - 2.0 * grow * alpha1 * m2 + alpha1 * alpha1 * m3
    alpha2 = norm1 / curv
    residual = beta_all - alpha1[:, None] * image_all
    direction = residual + ratio[:, None] * beta_all
    weights_all = alpha1[:, None] * beta_all + alpha2[:, None] * direction
    weights = lax.dynamic_slice_in_dim(weights_all, me_ind * traits_here, traits_here, 0)

    rounded = weights_all.astype(jnp.bfloat16)
    weights, rounded = lax.optimization_barrier((weights, rounded))
    partial = lax.dot_general(
        rounded, genotypes, (((1,), (1,)), ((), ())), preferred_element_type=jnp.float32
    )
    inds_here = genotypes.shape[0]
    share = inds_here // n_snp
    chunks = partial.reshape(traits, n_snp, share).transpose(1, 0, 2)
    complete = jnp.sum(lax.all_to_all(chunks, "snp", 0, 0, tiled=True), axis=0)
    count = inds_here * n_ind
    local_sum = jnp.sum(complete, axis=1)
    local_centred = complete - (local_sum / share)[:, None]
    local_square = jnp.sum(local_centred * local_centred, axis=1)
    both = jnp.stack([local_sum, local_square])
    sent = jnp.broadcast_to(both[None], (n_all,) + both.shape)
    every = lax.all_to_all(sent, ("ind", "snp"), 0, 0, tiled=True)
    average = jnp.sum(every[:, 0], axis=0) / count
    spread = every[:, 0] / share - average[None, :]
    squares = jnp.sum(every[:, 1], axis=0) + share * jnp.sum(spread * spread, axis=0)
    variance = squares / count
    centred = complete - average[:, None]
    scores = centred * lax.rsqrt(variance + 1e-05)[:, None]
    return (weights, scores)


def solution(mesh):
    placed = (P("ind", "snp"), P("snp", None), P("snp"), P("ind"), P("ind", "snp"))
    return jax.shard_map(
        local,
        mesh=mesh,
        in_specs=placed,
        out_specs=(P("ind", "snp"), P(None, ("ind", "snp"))),
        check_vma=False,
    )
```

```python
import jax
import jax.numpy as jnp
from jax import lax
from jax.sharding import PartitionSpec as P

BLK = 128
ITERS = 2
M_GENOME = 1100000
N_GWAS = 1000000
REACH = 416
SHIFT_BITS = 7


def all_sum(x, axes, count):
    sent = jnp.broadcast_to(x[None], (count,) + x.shape)
    return jnp.sum(lax.all_to_all(sent, axes, 0, 0, tiled=True), axis=0)


def windows_of(padded, shifts, band_cols, blocks_here):
    span = band_cols + (1 << SHIFT_BITS) - 1
    need = (blocks_here - 1) * BLK + span
    padded = jnp.pad(padded, ((0, 0), (0, max(0, need - padded.shape[1]))))
    wide = jnp.stack([padded[:, b * BLK : b * BLK + span] for b in range(blocks_here)])
    for bit in range(SHIFT_BITS):
        step = 1 << bit
        take = ((shifts >> bit) & 1)[:, None, None] == 1
        wide = jnp.where(take, wide[:, :, step:], wide[:, :, :-step])
    return wide[:, :, :band_cols]


def apply_operator(extended, vector, ld_band, shifts, ridge_shift):
    band_cols = ld_band.shape[1]
    blocks_here = ld_band.shape[0] // BLK
    windows = windows_of(extended, shifts, band_cols, blocks_here)
    blocks = ld_band.reshape(blocks_here, BLK, band_cols)
    product = jnp.einsum("btk,brk->tbr", windows, blocks, precision=lax.Precision.HIGH)
    return product.reshape(vector.shape)


def spread_operator(vector, ld_band, shifts, ridge_shift, halo):
    band_cols = ld_band.shape[1]
    blocks_here = ld_band.shape[0] // BLK
    traits, rows = vector.shape
    span = band_cols + (1 << SHIFT_BITS) - 1
    blocks = ld_band.reshape(blocks_here, BLK, band_cols)
    pieces = jnp.einsum(
        "tbr,brk->btk", vector.reshape(traits, blocks_here, BLK), blocks,
        precision=lax.Precision.HIGH,
    )
    wide = jnp.pad(pieces, ((0, 0), (0, 0), (0, span - band_cols)))
    for bit in range(SHIFT_BITS):
        step = 1 << bit
        take = ((shifts >> bit) & 1)[:, None, None] == 1
        moved = jnp.pad(wide, ((0, 0), (0, 0), (step, 0)))[:, :, :span]
        wide = jnp.where(take, moved, wide)
    width = max((blocks_here - 1) * BLK + span, rows + 2 * halo)
    own = sum(
        jnp.pad(wide[b], ((0, 0), (b * BLK, width - b * BLK - span))) for b in range(blocks_here)
    )[:, : rows + 2 * halo]
    own = own + jnp.pad(ridge_shift[:, None] * vector, ((0, 0), (halo, halo)))
    count = lax.axis_size("snp")
    forward = [(i, i + 1) for i in range(count - 1)]
    backward = [(target, source) for source, target in forward]
    from_left = lax.ppermute(own[:, rows:], "snp", forward)
    from_right = lax.ppermute(own[:, : 2 * halo], "snp", backward)
    return own, jnp.pad(from_left, ((0, 0), (0, rows))), jnp.pad(from_right, ((0, 0), (rows, 0)))


def local(beta_hat, ld_band, band_start, heritability, genotypes):
    n_snp = lax.axis_size("snp")
    n_ind = lax.axis_size("ind")
    n_all = n_snp * n_ind
    traits_here, rows_here = beta_hat.shape
    traits = traits_here * n_ind
    halo = ld_band.shape[1] - BLK - REACH
    offsets = band_start - lax.axis_index("snp") * rows_here + halo
    shifts = offsets - jnp.arange(band_start.shape[0], dtype=jnp.int32) * BLK

    ridge_shift = M_GENOME / N_GWAS / heritability
    own, left, right = spread_operator(beta_hat, ld_band, shifts, ridge_shift, halo)
    early = own + left
    image = (early + right)[:, halo : halo + rows_here]
    image2 = (
        apply_operator(early, image, ld_band, shifts, ridge_shift)
        + apply_operator(right, image, ld_band, shifts, ridge_shift)
    ) + ridge_shift[:, None] * image

    moments = jnp.stack(
        [
            jnp.sum(beta_hat * beta_hat, axis=1),
            jnp.sum(beta_hat * image, axis=1),
            jnp.sum(image * image, axis=1),
            jnp.sum(image * image2, axis=1),
        ]
    )
    m0, m1, m2, m3 = all_sum(moments, "snp", n_snp)

    alpha1 = m0 / m1
    norm1 = alpha1 * alpha1 * m2 - m0
    ratio = norm1 / m0
    grow = 1.0 + ratio
    curv = grow * grow * m1 - 2.0 * grow * alpha1 * m2 + alpha1 * alpha1 * m3
    alpha2 = norm1 / curv
    residual = beta_hat - alpha1[:, None] * image
    direction = residual + ratio[:, None] * beta_hat
    weights = alpha1[:, None] * beta_hat + alpha2[:, None] * direction

    rounded = lax.all_gather(weights.astype(jnp.bfloat16), "ind", axis=0, tiled=True)
    partial = lax.dot_general(
        rounded, genotypes, (((1,), (1,)), ((), ())), preferred_element_type=jnp.float32
    )
    inds_here = genotypes.shape[0]
    share = inds_here // n_snp
    chunks = partial.reshape(traits, n_snp, share).transpose(1, 0, 2)
    complete = jnp.sum(lax.all_to_all(chunks, "snp", 0, 0, tiled=True), axis=0)
    count = inds_here * n_ind
    local_sum = jnp.sum(complete, axis=1)
    local_centred = complete - (local_sum / share)[:, None]
    local_square = jnp.sum(local_centred * local_centred, axis=1)
    both = jnp.stack([local_sum, local_square])
    sent = jnp.broadcast_to(both[None], (n_all,) + both.shape)
    every = lax.all_to_all(sent, ("ind", "snp"), 0, 0, tiled=True)
    average = jnp.sum(every[:, 0], axis=0) / count
    spread = every[:, 0] / share - average[None, :]
    squares = jnp.sum(every[:, 1], axis=0) + share * jnp.sum(spread * spread, axis=0)
    variance = squares / count
    centred = complete - average[:, None]
    scores = centred * lax.rsqrt(variance + 1e-05)[:, None]
    return (weights, scores)


def solution(mesh):
    placed = (P("ind", "snp"), P("snp", None), P("snp"), P("ind"), P("ind", "snp"))
    return jax.shard_map(
        local,
        mesh=mesh,
        in_specs=placed,
        out_specs=(P("ind", "snp"), P(None, ("ind", "snp"))),
        check_vma=False,
    )
```

```python
import jax
import jax.numpy as jnp
from jax import lax
from jax.sharding import PartitionSpec as P

BLK = 128
ITERS = 2
M_GENOME = 1100000
N_GWAS = 1000000
REACH = 416
SHIFT_BITS = 7


def all_sum(x, axes, count):
    sent = jnp.broadcast_to(x[None], (count,) + x.shape)
    return jnp.sum(lax.all_to_all(sent, axes, 0, 0, tiled=True), axis=0)


def windows_of(padded, shifts, band_cols, blocks_here):
    span = band_cols + (1 << SHIFT_BITS) - 1
    need = (blocks_here - 1) * BLK + span
    padded = jnp.pad(padded, ((0, 0), (0, max(0, need - padded.shape[1]))))
    wide = jnp.stack([padded[:, b * BLK : b * BLK + span] for b in range(blocks_here)])
    for bit in range(SHIFT_BITS):
        step = 1 << bit
        take = ((shifts >> bit) & 1)[:, None, None] == 1
        wide = jnp.where(take, wide[:, :, step:], wide[:, :, :-step])
    return wide[:, :, :band_cols]


def apply_operator(extended, vector, ld_band, shifts, ridge_shift):
    band_cols = ld_band.shape[1]
    blocks_here = ld_band.shape[0] // BLK
    windows = windows_of(extended, shifts, band_cols, blocks_here)
    blocks = ld_band.reshape(blocks_here, BLK, band_cols)
    product = jnp.einsum("btk,brk->tbr", windows, blocks, precision=lax.Precision.HIGH)
    return product.reshape(vector.shape) + ridge_shift[:, None] * vector


def spread_operator(vector, ld_band, shifts, ridge_shift, halo):
    band_cols = ld_band.shape[1]
    blocks_here = ld_band.shape[0] // BLK
    traits, rows = vector.shape
    span = band_cols + (1 << SHIFT_BITS) - 1
    blocks = ld_band.reshape(blocks_here, BLK, band_cols)
    pieces = jnp.einsum(
        "tbr,brk->btk", vector.reshape(traits, blocks_here, BLK), blocks,
        precision=lax.Precision.HIGH,
    )
    wide = jnp.pad(pieces, ((0, 0), (0, 0), (0, span - band_cols)))
    for bit in range(SHIFT_BITS):
        step = 1 << bit
        take = ((shifts >> bit) & 1)[:, None, None] == 1
        moved = jnp.pad(wide, ((0, 0), (0, 0), (step, 0)))[:, :, :span]
        wide = jnp.where(take, moved, wide)
    width = max((blocks_here - 1) * BLK + span, rows + 2 * halo)
    own = sum(
        jnp.pad(wide[b], ((0, 0), (b * BLK, width - b * BLK - span))) for b in range(blocks_here)
    )[:, : rows + 2 * halo]
    own = own + jnp.pad(ridge_shift[:, None] * vector, ((0, 0), (halo, halo)))
    count = lax.axis_size("snp")
    forward = [(i, i + 1) for i in range(count - 1)]
    backward = [(target, source) for source, target in forward]
    from_left = lax.ppermute(own[:, rows:], "snp", forward)
    from_right = lax.ppermute(own[:, : 2 * halo], "snp", backward)
    return own + jnp.pad(from_left, ((0, 0), (0, rows))) + jnp.pad(from_right, ((0, 0), (rows, 0)))


def local(beta_hat, ld_band, band_start, heritability, genotypes):
    n_snp = lax.axis_size("snp")
    n_ind = lax.axis_size("ind")
    n_all = n_snp * n_ind
    traits_here, rows_here = beta_hat.shape
    traits = traits_here * n_ind
    halo = ld_band.shape[1] - BLK - REACH
    offsets = band_start - lax.axis_index("snp") * rows_here + halo
    shifts = offsets - jnp.arange(band_start.shape[0], dtype=jnp.int32) * BLK

    ridge_shift = M_GENOME / N_GWAS / heritability
    extended = spread_operator(beta_hat, ld_band, shifts, ridge_shift, halo)
    image = extended[:, halo : halo + rows_here]
    image2 = apply_operator(extended, image, ld_band, shifts, ridge_shift)

    moments = jnp.stack(
        [
            jnp.sum(beta_hat * beta_hat, axis=1),
            jnp.sum(beta_hat * image, axis=1),
            jnp.sum(image * image, axis=1),
            jnp.sum(image * image2, axis=1),
        ]
    )
    m0, m1, m2, m3 = all_sum(moments.reshape(-1), "snp", n_snp).reshape(moments.shape)

    alpha1 = m0 / m1
    norm1 = alpha1 * alpha1 * m2 - m0
    ratio = norm1 / m0
    grow = 1.0 + ratio
    curv = grow * grow * m1 - 2.0 * grow * alpha1 * m2 + alpha1 * alpha1 * m3
    alpha2 = norm1 / curv
    residual = beta_hat - alpha1[:, None] * image
    direction = residual + ratio[:, None] * beta_hat
    weights = alpha1[:, None] * beta_hat + alpha2[:, None] * direction

    rounded = lax.all_gather(weights.astype(jnp.bfloat16), "ind", axis=0, tiled=True)
    partial = lax.dot_general(
        rounded, genotypes, (((1,), (1,)), ((), ())), preferred_element_type=jnp.float32
    )
    inds_here = genotypes.shape[0]
    share = inds_here // n_snp
    chunks = partial.reshape(traits, n_snp, share).transpose(1, 0, 2)
    complete = jnp.sum(lax.all_to_all(chunks, "snp", 0, 0, tiled=True), axis=0)
    count = inds_here * n_ind
    local_sum = jnp.sum(complete, axis=1)
    local_centred = complete - (local_sum / share)[:, None]
    local_square = jnp.sum(local_centred * local_centred, axis=1)
    both = jnp.stack([local_sum, local_square])
    sent = jnp.broadcast_to(both[None], (n_all,) + both.shape)
    every = lax.all_to_all(sent, ("ind", "snp"), 0, 0, tiled=True)
    average = jnp.sum(every[:, 0], axis=0) / count
    spread = every[:, 0] / share - average[None, :]
    squares = jnp.sum(every[:, 1], axis=0) + share * jnp.sum(spread * spread, axis=0)
    variance = squares / count
    centred = complete - average[:, None]
    scores = centred * lax.rsqrt(variance + 1e-05)[:, None]
    return (weights, scores)


def solution(mesh):
    placed = (P("ind", "snp"), P("snp", None), P("snp"), P("ind"), P("ind", "snp"))
    return jax.shard_map(
        local,
        mesh=mesh,
        in_specs=placed,
        out_specs=(P("ind", "snp"), P(None, ("ind", "snp"))),
        check_vma=False,
    )
```

```python
import jax
import jax.numpy as jnp
from jax import lax
from jax.sharding import PartitionSpec as P

BLK = 128
ITERS = 2
M_GENOME = 1100000
N_GWAS = 1000000
REACH = 416
SHIFT_BITS = 7


def all_sum(x, axes, count):
    sent = jnp.broadcast_to(x[None], (count,) + x.shape)
    return jnp.sum(lax.all_to_all(sent, axes, 0, 0, tiled=True), axis=0)


def windows_of(padded, shifts, band_cols, blocks_here):
    span = band_cols + (1 << SHIFT_BITS) - 1
    need = (blocks_here - 1) * BLK + span
    padded = jnp.pad(padded, ((0, 0), (0, max(0, need - padded.shape[1]))))
    wide = jnp.stack([padded[:, b * BLK : b * BLK + span] for b in range(blocks_here)])
    for bit in range(SHIFT_BITS):
        step = 1 << bit
        take = ((shifts >> bit) & 1)[:, None, None] == 1
        wide = jnp.where(take, wide[:, :, step:], wide[:, :, :-step])
    return wide[:, :, :band_cols]


def apply_operator(extended, vector, ld_band, shifts, ridge_shift):
    band_cols = ld_band.shape[1]
    blocks_here = ld_band.shape[0] // BLK
    windows = windows_of(extended, shifts, band_cols, blocks_here)
    blocks = ld_band.reshape(blocks_here, BLK, band_cols)
    product = jnp.einsum("btk,brk->tbr", windows, blocks, precision=lax.Precision.HIGH)
    return product.reshape(vector.shape) + ridge_shift[:, None] * vector


def spread_operator(vector, ld_band, shifts, ridge_shift, halo):
    band_cols = ld_band.shape[1]
    blocks_here = ld_band.shape[0] // BLK
    traits, rows = vector.shape
    span = band_cols + (1 << SHIFT_BITS) - 1
    blocks = ld_band.reshape(blocks_here, BLK, band_cols)
    pieces = jnp.einsum(
        "tbr,brk->btk", vector.reshape(traits, blocks_here, BLK), blocks,
        precision=lax.Precision.HIGH,
    )
    pieces, shifts = lax.optimization_barrier((pieces, shifts))
    wide = jnp.pad(pieces, ((0, 0), (0, 0), (0, span - band_cols)))
    for bit in range(SHIFT_BITS):
        step = 1 << bit
        take = ((shifts >> bit) & 1)[:, None, None] == 1
        moved = jnp.pad(wide, ((0, 0), (0, 0), (step, 0)))[:, :, :span]
        wide = jnp.where(take, moved, wide)
    width = max((blocks_here - 1) * BLK + span, rows + 2 * halo)
    own = sum(
        jnp.pad(wide[b], ((0, 0), (b * BLK, width - b * BLK - span))) for b in range(blocks_here)
    )[:, : rows + 2 * halo]
    own = own + jnp.pad(ridge_shift[:, None] * vector, ((0, 0), (halo, halo)))
    count = lax.axis_size("snp")
    forward = [(i, i + 1) for i in range(count - 1)]
    backward = [(target, source) for source, target in forward]
    from_left = lax.ppermute(own[:, rows:], "snp", forward)
    from_right = lax.ppermute(own[:, : 2 * halo], "snp", backward)
    total = own + jnp.pad(from_left, ((0, 0), (0, rows))) + jnp.pad(from_right, ((0, 0), (rows, 0)))
    return total, shifts


def local(beta_hat, ld_band, band_start, heritability, genotypes):
    n_snp = lax.axis_size("snp")
    n_ind = lax.axis_size("ind")
    n_all = n_snp * n_ind
    traits_here, rows_here = beta_hat.shape
    traits = traits_here * n_ind
    halo = ld_band.shape[1] - BLK - REACH
    offsets = band_start - lax.axis_index("snp") * rows_here + halo
    shifts = offsets - jnp.arange(band_start.shape[0], dtype=jnp.int32) * BLK

    ridge_shift = M_GENOME / N_GWAS / heritability
    extended, shifts = spread_operator(beta_hat, ld_band, shifts, ridge_shift, halo)
    image = extended[:, halo : halo + rows_here]
    image2 = apply_operator(extended, image, ld_band, shifts, ridge_shift)

    moments = jnp.stack(
        [
            jnp.sum(beta_hat * beta_hat, axis=1),
            jnp.sum(beta_hat * image, axis=1),
            jnp.sum(image * image, axis=1),
            jnp.sum(image * image2, axis=1),
        ]
    )
    m0, m1, m2, m3 = all_sum(moments, "snp", n_snp)

    alpha1 = m0 / m1
    norm1 = alpha1 * alpha1 * m2 - m0
    ratio = norm1 / m0
    grow = 1.0 + ratio
    curv = grow * grow * m1 - 2.0 * grow * alpha1 * m2 + alpha1 * alpha1 * m3
    alpha2 = norm1 / curv
    residual = beta_hat - alpha1[:, None] * image
    direction = residual + ratio[:, None] * beta_hat
    weights = alpha1[:, None] * beta_hat + alpha2[:, None] * direction

    rounded = lax.all_gather(weights.astype(jnp.bfloat16), "ind", axis=0, tiled=True)
    partial = lax.dot_general(
        rounded, genotypes, (((1,), (1,)), ((), ())), preferred_element_type=jnp.float32
    )
    inds_here = genotypes.shape[0]
    share = inds_here // n_snp
    chunks = partial.reshape(traits, n_snp, share).transpose(1, 0, 2)
    complete = jnp.sum(lax.all_to_all(chunks, "snp", 0, 0, tiled=True), axis=0)
    count = inds_here * n_ind
    local_sum = jnp.sum(complete, axis=1)
    local_centred = complete - (local_sum / share)[:, None]
    local_square = jnp.sum(local_centred * local_centred, axis=1)
    both = jnp.stack([local_sum, local_square])
    sent = jnp.broadcast_to(both[None], (n_all,) + both.shape)
    every = lax.all_to_all(sent, ("ind", "snp"), 0, 0, tiled=True)
    average = jnp.sum(every[:, 0], axis=0) / count
    spread = every[:, 0] / share - average[None, :]
    squares = jnp.sum(every[:, 1], axis=0) + share * jnp.sum(spread * spread, axis=0)
    variance = squares / count
    centred = complete - average[:, None]
    scores = centred * lax.rsqrt(variance + 1e-05)[:, None]
    return (weights, scores)


def solution(mesh):
    placed = (P("ind", "snp"), P("snp", None), P("snp"), P("ind"), P("ind", "snp"))
    return jax.shard_map(
        local,
        mesh=mesh,
        in_specs=placed,
        out_specs=(P("ind", "snp"), P(None, ("ind", "snp"))),
        check_vma=False,
    )
```
